32 devices in a mesh: tensor: 2 (over y), req: 4 (over z), seq: 4 (over x, core).
Axes of the slice: x: 2, y: 2, z: 4, core: 2. Of those that a mesh axis runs over, the one named last changes fastest.
Arguments:
- draft_query: bfloat16 [4, 64, 8192], P('req', None, 'tensor'), may hold values from -6 to 6
- draft_kv: bfloat16 [4, 2, 64, 1024], P('req', None, None, 'tensor'), may hold values from -6 to 6
- own_cache: bfloat16 [4, 2, 32768, 1024], P('req', None, 'seq', 'tensor'), may hold values from -6 to 6
- shared_cache: bfloat16 [2, 2, 8192, 1024], P(None, None, ('req', 'seq'), 'tensor'), may hold values from -6 to 6
- out_weight: bfloat16 [8192, 8192], P(('tensor', 'seq')), may hold values from -0.09375 to 0.09375
- lengths: int32 [4], P('req'), may hold values from 1 to 32768, as said below
- group_ids: int32 [4], replicated, may hold values from 0 to 1
- parents: int32 [4, 64], P('req'), may hold values from -1 to 62, as said below
- accepted: int32 [4, 8], P('req'), may hold values from 0 to 62, as said below
Outputs:
- verified: bfloat16 [4, 64, 8192], P('req', None, ('tensor', 'seq'))
- accepted_kv: bfloat16 [4, 2, 8, 1024], P('req', None, None, 'tensor')
The draws below stay inside these ranges and needn't reach their ends.
Inputs may be any that keep to these rules, and one draw needn't show every extreme that they name: Request r attends to own cache positions 0 to lengths[r] - 1; some request has exactly 32768. parents[r, 0] = -1 and 0 <= parents[r, i] < i for i >= 1. accepted[r, 0] = 0 and parents[r, accepted[r, a]] = accepted[r, a - 1]: a path from the root.
All inputs are finite; a program needn't handle non-finite values.
Results may differ from the reference program's by a relative error of at most 0.012.
Values may be sent and summed in bfloat16 or wider, within the bound.
No kernel may reach another device: no remote copies, remote signals or barrier semaphores. Data moves between devices by JAX's collectives and lax.ppermute only.
A program may use at most 192 MiB of HBM per device.

```python
import jax
import jax.numpy as jnp
from jax import lax

D = 8192
HQ = 64
KVH = 8
HD = 128
QPK = 8
DRAFT = 64
PATH = 8
GROUPS = 2
REQS = 4
PROMPT = 8192
MAXLEN = 32768


def draw_draft_query(key, part):
    shape = (REQS, DRAFT, HQ * HD)
    base_key = jax.random.fold_in(key, 11)
    values = jnp.clip(jax.random.normal(base_key, shape, jnp.float32), -6.0, 6.0)
    return values.astype(jnp.bfloat16)


def draw_shared_cache(key, part):
    shape = (2, GROUPS, PROMPT, KVH * HD)
    base_key = jax.random.fold_in(key, 17)
    values = jnp.clip(jax.random.normal(base_key, shape, jnp.float32), -6.0, 6.0)
    return values.astype(jnp.bfloat16)


def draw_lengths(key, part):
    drawn = jax.random.randint(jax.random.fold_in(key, 21), (REQS,), 1, MAXLEN + 1)
    longest = jax.random.randint(jax.random.fold_in(key, 22), (), 0, REQS)
    step_over = jax.random.randint(jax.random.fold_in(key, 23), (), 1, REQS)
    shortest = (longest + step_over) % REQS
    drawn = drawn.at[longest].set(MAXLEN)
    drawn = drawn.at[shortest].set(1)
    return drawn.astype(jnp.int32)


def one_tree(tree_key, forced):
    order = jax.random.permutation(jax.random.fold_in(tree_key, 1), DRAFT - 2).astype(jnp.int32) + 1
    chosen = jnp.sort(order[:PATH - 1])
    chosen = jnp.where(forced, chosen.at[PATH - 2].set(DRAFT - 2), chosen)
    path_nodes = jnp.concatenate([jnp.zeros((1,), jnp.int32), chosen])
    nodes = jnp.arange(DRAFT, dtype=jnp.int32)
    parent_row = jax.random.randint(jax.random.fold_in(tree_key, 2), (DRAFT,), 0, jnp.maximum(nodes, 1))
    parent_row = parent_row.astype(jnp.int32).at[DRAFT - 1].set(DRAFT - 2)
    parent_row = parent_row.at[chosen].set(path_nodes[:-1])
    parent_row = parent_row.at[0].set(-1)
    return (parent_row, path_nodes)


def tree_draw(key):
    tree_keys = jax.random.split(jax.random.fold_in(key, 31), REQS)
    forced_row = jax.random.randint(jax.random.fold_in(key, 32), (), 0, REQS)
    forced = jnp.arange(REQS, dtype=jnp.int32) == forced_row
    return jax.vmap(one_tree)(tree_keys, forced)


def draw_parents(key, part):
    return tree_draw(key)[0]


def draw_accepted(key, part):
    return tree_draw(key)[1]


def with_ends(entries, key, smallest, largest):
    spot = [jax.random.randint(jax.random.fold_in(key, axis), (), 0, length) for axis, length in enumerate(entries.shape)]
    widest = entries.shape.index(max(entries.shape))
    neighbour = spot[:widest] + [(spot[widest] + 1) % entries.shape[widest]] + spot[widest + 1:]
    return entries.at[tuple(spot)].set(smallest).at[tuple(neighbour)].set(largest)


def spiked(result, rng, source, target, shards_of, factor):
    owner, partner = [(jnp.arange(result.shape[axis_at]) // (result.shape[axis_at] // shards_of)).reshape([-1 if axis == axis_at else 1 for axis in range(result.ndim)]) for axis_at in (source, target)]
    chosen = jax.random.permutation(rng, shards_of)[partner]
    strong = (owner == chosen) | (owner == (partner + shards_of // 2) % shards_of)
    return jnp.where(strong, factor * result, result)


def block_scale(rng, extent, cuts, least, high):
    def one(dim, parts):
        draws = jax.random.uniform(jax.random.fold_in(jax.random.fold_in(rng, 6), dim), (parts,), jnp.float32, least / len(cuts), high / len(cuts))
        return jnp.repeat(jnp.exp(draws), extent[dim] // parts).reshape((-1,) + (1,) * (len(extent) - dim - 1))

    gain = one(*cuts[0])
    for cut in cuts[1:]:
        gain = gain * one(*cut)
    return gain


def normal_values(stream_key, dims, deviation, most, cuts=(), held_as=jnp.bfloat16):
    values = deviation * jax.random.normal(stream_key, dims, jnp.float32)
    if cuts:
        values = values * block_scale(stream_key, dims, cuts, -0.22, 0.18)
    return jnp.clip(values, -most, most).astype(held_as)


def noise_with(key, dims, deviation, limit, cuts, heavy, kind=jnp.bfloat16):
    values = deviation * jax.random.normal(key, dims, jnp.float32)
    if cuts:
        values = values * block_scale(key, dims, cuts, -0.22, 0.18)
    return jnp.clip(spiked(values, jax.random.fold_in(key, 3), *heavy), -limit, limit).astype(kind)


def setup_inputs(seed: int = 0) -> dict:
    streams_of = jax.random.split(jax.random.key(seed), 10)
    return {
        "draft_query": draw_draft_query(jax.random.fold_in(streams_of[9], 71), 0),
        "draft_kv": normal_values(streams_of[1], (REQS, 2, DRAFT, KVH * HD), 1.0, 6.0, ((0, 4), (3, 2))),
        "own_cache": normal_values(streams_of[2], (REQS, 2, MAXLEN, KVH * HD), 1.0, 6.0, ((0, 4), (2, 4), (3, 2))),
        "shared_cache": draw_shared_cache(jax.random.fold_in(streams_of[9], 71), 0),
        "out_weight": noise_with(streams_of[4], (HQ * HD, D), (HQ * HD) ** -0.5, 0.09375, ((0, 8),), (0, 1, 8, 2.0)),
        "lengths": draw_lengths(jax.random.fold_in(streams_of[9], 71), 0),
        "group_ids": with_ends(jax.random.randint(streams_of[6], (REQS,), 0, 2), jax.random.fold_in(streams_of[6], 1), 0, 1).astype(jnp.int32),
        "parents": draw_parents(jax.random.fold_in(streams_of[9], 71), 0),
        "accepted": draw_accepted(jax.random.fold_in(streams_of[9], 71), 0),
    }


NEG_FILL = -1e30


def tree_reach(parent_row):
    node_count = parent_row.shape[0]
    nodes = jnp.arange(node_count, dtype=jnp.int32)
    reach = jnp.eye(node_count, dtype=jnp.float32) + (parent_row[:, None] == nodes[None, :]).astype(jnp.float32)
    for level_step in range(max(node_count - 1, 1).bit_length()):
        reach = jnp.minimum(jnp.dot(reach, reach, precision=lax.Precision.HIGHEST), 1.0)
    return reach > 0.5


def reference(draft_query, draft_kv, own_cache, shared_cache, out_weight, lengths, group_ids, parents, accepted):
    score_scale = HD ** -0.5

    def one_request(request):
        reach = tree_reach(parents[request])
        queries = draft_query[request].reshape(DRAFT, KVH, QPK, HD)
        shared = lax.dynamic_index_in_dim(shared_cache, group_ids[request], 1, keepdims=False)
        all_keys = jnp.concatenate([shared[0], own_cache[request, 0], draft_kv[request, 0]], 0).reshape(-1, KVH, HD)
        all_values = jnp.concatenate([shared[1], own_cache[request, 1], draft_kv[request, 1]], 0).reshape(-1, KVH, HD)
        live = jnp.arange(MAXLEN, dtype=jnp.int32) < lengths[request]
        key_ok = jnp.concatenate([
            jnp.ones((QPK * DRAFT, PROMPT), jnp.bool_),
            jnp.broadcast_to(live[None, :], (QPK * DRAFT, MAXLEN)),
            jnp.tile(reach, (QPK, 1))], 1)

        def one_head(head):
            head_query = lax.dynamic_index_in_dim(queries, head, 1, keepdims=False)
            query_rows = jnp.transpose(head_query, (1, 0, 2)).reshape(QPK * DRAFT, HD)
            head_keys = lax.dynamic_index_in_dim(all_keys, head, 1, keepdims=False)
            head_values = lax.dynamic_index_in_dim(all_values, head, 1, keepdims=False)
            scores = jnp.dot(query_rows, head_keys.T, preferred_element_type=jnp.float32) * score_scale
            scores = jnp.where(key_ok, scores, NEG_FILL)
            row_max = jnp.max(scores, axis=1, keepdims=True)
            weights = jnp.where(key_ok, jnp.exp(scores - row_max), 0.0)
            total = jnp.sum(weights, axis=1, keepdims=True)
            summed = jnp.dot(weights.astype(jnp.bfloat16), head_values, preferred_element_type=jnp.float32) / total
            return summed.astype(jnp.bfloat16).reshape(QPK, DRAFT, HD)

        heads = lax.map(one_head, jnp.arange(KVH, dtype=jnp.int32))
        attended = jnp.transpose(heads, (2, 0, 1, 3)).reshape(DRAFT, HQ * HD)
        return jnp.dot(attended, out_weight, preferred_element_type=jnp.float32).astype(jnp.bfloat16)

    verified = lax.map(one_request, jnp.arange(REQS, dtype=jnp.int32))

    def pick_path(request_kv, path_row):
        return jnp.take(request_kv, path_row, axis=1)

    accepted_kv = jax.vmap(pick_path)(draft_kv, accepted)
    return verified, accepted_kv
```

```python
import functools

import jax
import jax.numpy as jnp
from jax import lax
from jax.experimental import pallas as pl
from jax.experimental.pallas import tpu as pltpu
from jax.sharding import PartitionSpec as P

HD = 128
QPK = 8
NEG_FILL = -1e30
SCALE = HD ** (-0.5)
OWN_BLOCK = 512


def step(m_prev, l_prev, acc_prev, q, k, v, ok):
    scores = lax.dot_general(
        q, k, (((1,), (1,)), ((), ())), preferred_element_type=jnp.float32
    ) * SCALE
    if ok is not None:
        scores = jnp.where(ok, scores, NEG_FILL)
    m_new = jnp.maximum(m_prev, jnp.max(scores, axis=1, keepdims=True))
    alpha = jnp.exp(m_prev - m_new)
    weights = jnp.exp(scores - m_new)
    if ok is not None:
        weights = jnp.where(ok, weights, 0.0)
    l_new = alpha * l_prev + jnp.sum(weights, axis=1, keepdims=True)
    acc_new = alpha * acc_prev + jnp.dot(
        weights.astype(jnp.bfloat16), v, preferred_element_type=jnp.float32
    )
    return m_new, l_new, acc_new


def own_kernel(kv_heads, block, nv_ref, q_ref, kv_ref, m_out, l_out, acc_out, m_s, l_s, acc_s):
    j = pl.program_id(0)
    n_valid = nv_ref[0]

    @pl.when(j == 0)
    def _():
        m_s[...] = jnp.full(m_s.shape, NEG_FILL, jnp.float32)
        l_s[...] = jnp.zeros(l_s.shape, jnp.float32)
        acc_s[...] = jnp.zeros(acc_s.shape, jnp.float32)

    start = j * block

    def body(masked):
        ok = None
        if masked:
            cols = start + lax.broadcasted_iota(jnp.int32, (1, block), 1)
            ok = cols < n_valid
        for h in range(kv_heads):
            cols_h = slice(h * HD, (h + 1) * HD)
            m, l, acc = step(
                m_s[h], l_s[h], acc_s[h], q_ref[h], kv_ref[0, :, cols_h], kv_ref[1, :, cols_h], ok
            )
            m_s[h] = m
            l_s[h] = l
            acc_s[h] = acc

    full = start + block <= n_valid
    part = jnp.logical_and(start < n_valid, jnp.logical_not(full))
    pl.when(full)(lambda: body(False))
    pl.when(part)(lambda: body(True))

    @pl.when(j == pl.num_programs(0) - 1)
    def _():
        m_out[...] = m_s[...]
        l_out[...] = l_s[...]
        acc_out[...] = acc_s[...]


def own_attend(q, kv, n_valid):
    kv_heads, rows, _ = q.shape
    cache_len = kv.shape[1]
    block = min(OWN_BLOCK, cache_len)
    n_blocks = cache_len // block

    def kv_map(j, nv):
        last = jnp.maximum((nv[0] + block - 1) // block - 1, 0)
        return (0, jnp.minimum(j, last), 0)

    state_shapes = (
        jax.ShapeDtypeStruct((kv_heads, rows, 1), jnp.float32),
        jax.ShapeDtypeStruct((kv_heads, rows, 1), jnp.float32),
        jax.ShapeDtypeStruct((kv_heads, rows, HD), jnp.float32),
    )
    full3 = lambda j, nv: (0, 0, 0)
    return pl.pallas_call(
        functools.partial(own_kernel, kv_heads, block),
        out_shape=state_shapes,
        grid_spec=pltpu.PrefetchScalarGridSpec(
            num_scalar_prefetch=1,
            grid=(n_blocks,),
            in_specs=[
                pl.BlockSpec(q.shape, full3),
                pl.BlockSpec((2, block, kv.shape[2]), kv_map),
            ],
            out_specs=[pl.BlockSpec(s.shape, full3) for s in state_shapes],
            scratch_shapes=[pltpu.VMEM(s.shape, jnp.float32) for s in state_shapes],
        ),
        compiler_params=pltpu.CompilerParams(dimension_semantics=("arbitrary",)),
        cost_estimate=pl.CostEstimate(
            flops=4 * kv_heads * rows * cache_len * HD,
            transcendentals=kv_heads * rows * cache_len,
            bytes_accessed=kv.size * 2 + q.size * 2,
        ),
    )(n_valid, q, kv)


def shared_kernel(kv_heads, n_blocks, flag_ref, q_ref, m_ref, l_ref, acc_ref, *rest):
    blocks = rest[:n_blocks]
    dkv_ref, reach_ref = rest[n_blocks], rest[n_blocks + 1]
    m_out, l_out, acc_out = rest[n_blocks + 2:n_blocks + 5]
    for h in range(kv_heads):
        cols_h = slice(h * HD, (h + 1) * HD)
        q = q_ref[h]
        m, l, acc = m_ref[h], l_ref[h], acc_ref[h]
        for blk in blocks:
            m, l, acc = step(m, l, acc, q, blk[0, :, cols_h], blk[1, :, cols_h], None)
        m_out[h] = m
        l_out[h] = l
        acc_out[h] = acc

    @pl.when(flag_ref[0] == 1)
    def _():
        ok = reach_ref[...] > 0.5
        for h in range(kv_heads):
            cols_h = slice(h * HD, (h + 1) * HD)
            m, l, acc = step(
                m_out[h], l_out[h], acc_out[h], q_ref[h],
                dkv_ref[0, :, cols_h], dkv_ref[1, :, cols_h], ok,
            )
            m_out[h] = m
            l_out[h] = l
            acc_out[h] = acc


def shared_attend(q, state, blocks, draft_kv, reach_rows, flag):
    kv_heads, rows, _ = q.shape
    n_blocks = len(blocks)
    whole = lambda a: pl.BlockSpec(a.shape, lambda i, f: (0,) * a.ndim)
    operands = (q,) + tuple(state) + tuple(blocks) + (draft_kv, reach_rows)
    keys = sum(b.shape[1] for b in blocks)
    return pl.pallas_call(
        functools.partial(shared_kernel, kv_heads, n_blocks),
        out_shape=tuple(jax.ShapeDtypeStruct(s.shape, s.dtype) for s in state),
        grid_spec=pltpu.PrefetchScalarGridSpec(
            num_scalar_prefetch=1,
            grid=(1,),
            in_specs=[whole(a) for a in operands],
            out_specs=[whole(s) for s in state],
        ),
        compiler_params=pltpu.CompilerParams(vmem_limit_bytes=48 * 1024 * 1024),
        cost_estimate=pl.CostEstimate(
            flops=4 * kv_heads * rows * keys * HD,
            transcendentals=kv_heads * rows * keys,
            bytes_accessed=sum(b.size * 2 for b in blocks) + q.size * 2,
        ),
    )(flag, *operands)


def tree_reach(parent_row):
    node_count = parent_row.shape[0]
    nodes = jnp.arange(node_count, dtype=jnp.int32)
    reach = jnp.eye(node_count, dtype=jnp.float32) + (parent_row[:, None] == nodes[None, :]).astype(
        jnp.float32
    )
    for level_step in range(max(node_count - 1, 1).bit_length()):
        reach = jnp.minimum(jnp.dot(reach, reach, precision=lax.Precision.HIGHEST), 1.0)
    return reach > 0.5


def exchange_shared(shared_cache, group_ids, req_index, req_count):
    local = shared_cache[:, group_ids[req_index]]
    received = [local]
    pow2 = req_count & (req_count - 1) == 0
    for k in range(1, req_count):
        if pow2:
            pairs = [(r, r ^ k) for r in range(req_count)]
            dst = req_index ^ k
        else:
            pairs = [(r, (r + k) % req_count) for r in range(req_count)]
            dst = (req_index + k) % req_count
        sent = lax.dynamic_index_in_dim(shared_cache, group_ids[dst], 1, keepdims=False)
        received.append(lax.ppermute(sent, "req", pairs))
    return received


def shards(
    draft_query,
    draft_kv,
    own_cache,
    shared_cache,
    out_weight,
    lengths,
    group_ids,
    parents,
    accepted,
):
    kv_heads = own_cache.shape[3] // HD
    draft_len = draft_query.shape[1]
    rows = QPK * draft_len
    seq_count = lax.axis_size("seq")
    seq_index = lax.axis_index("seq")
    req_index = lax.axis_index("req")
    req_count = lax.axis_size("req")
    cache_len = own_cache.shape[2]

    blocks = exchange_shared(shared_cache, group_ids, req_index, req_count)

    queries = (
        draft_query[0]
        .reshape(draft_len, kv_heads, QPK, HD)
        .transpose(1, 2, 0, 3)
        .reshape(kv_heads, rows, HD)
    )
    n_valid = jnp.clip(lengths[0] - seq_index * cache_len, 0, cache_len).astype(jnp.int32)
    state = own_attend(queries, own_cache[0], n_valid.reshape(1))

    reach = tree_reach(parents[0])
    reach_rows = jnp.tile(reach.astype(jnp.float32), (QPK, 1))
    flag = (seq_index == 0).astype(jnp.int32).reshape(1)
    m, l, acc = shared_attend(queries, state, blocks, draft_kv[0], reach_rows, flag)

    heads_dev = kv_heads * QPK
    share = heads_dev // seq_count
    stats = jnp.stack([m.reshape(heads_dev, draft_len), l.reshape(heads_dev, draft_len)], 0)
    stats = lax.all_to_all(stats, "seq", 1, 1, tiled=True).reshape(2, seq_count, share, draft_len)
    acc = lax.all_to_all(acc.reshape(heads_dev, draft_len, HD), "seq", 0, 0, tiled=True)
    acc = acc.reshape(seq_count, share, draft_len, HD)
    part_max, part_total = stats[0], stats[1]
    final_max = jnp.max(part_max, axis=0)
    factor = jnp.exp(part_max - final_max[None])
    final_total = jnp.sum(part_total * factor, axis=0)
    final_sum = jnp.sum(acc * factor[..., None], axis=0)
    attended = (final_sum / final_total[..., None]).astype(jnp.bfloat16)
    attended = jnp.transpose(attended, (1, 0, 2)).reshape(draft_len, share * HD)
    out_piece = lax.psum_scatter(
        lax.dot_general(
            out_weight, attended, (((0,), (1,)), ((), ())), preferred_element_type=jnp.float32
        ),
        ("tensor", "seq"),
        scatter_dimension=0,
        tiled=True,
    )
    verified = out_piece.T[None].astype(jnp.bfloat16)
    accepted_kv = jnp.take(draft_kv[0], accepted[0], axis=1)[None]
    return (verified, accepted_kv)


def solution(mesh):
    placed = (
        P("req", None, "tensor"),
        P("req", None, None, "tensor"),
        P("req", None, "seq", "tensor"),
        P(None, None, ("req", "seq"), "tensor"),
        P(("tensor", "seq"), None),
        P("req"),
        P(),
        P("req", None),
        P("req", None),
    )
    return jax.shard_map(
        shards,
        mesh=mesh,
        in_specs=placed,
        out_specs=(P("req", None, ("tensor", "seq")), P("req", None, None, "tensor")),
        check_vma=False,
    )
```

```python
import functools

import jax
import jax.numpy as jnp
from jax import lax
from jax.experimental import pallas as pl
from jax.experimental.pallas import tpu as pltpu
from jax.sharding import PartitionSpec as P

HD = 128
QPK = 8
NEG_FILL = -1e30
SCALE = HD ** (-0.5)
EXP2_SCALE = SCALE * 1.4426950408889634
OWN_BLOCK = 512


def step(m_prev, l_prev, acc_prev, q, k, v, ones, ok):
    scores = lax.dot_general(
        q, k, (((1,), (1,)), ((), ())), preferred_element_type=jnp.float32
    )
    if ok is not None:
        scores = jnp.where(ok, scores, NEG_FILL)
    m_new = jnp.maximum(m_prev, jnp.max(scores, axis=1, keepdims=True))
    alpha = jnp.exp2((m_prev - m_new) * EXP2_SCALE)
    weights = jnp.exp2((scores - m_new) * EXP2_SCALE)
    if ok is not None:
        weights = jnp.where(ok, weights, 0.0)
    weights = weights.astype(jnp.bfloat16)
    l_new = alpha * l_prev + jnp.dot(weights, ones, preferred_element_type=jnp.float32)
    acc_new = alpha * acc_prev + jnp.dot(weights, v, preferred_element_type=jnp.float32)
    return m_new, l_new, acc_new


def own_kernel(kv_heads, block, nv_ref, q_ref, kv_ref, ones_ref, m_out, l_out, acc_out, m_s, l_s, acc_s):
    j = pl.program_id(0)
    n_valid = nv_ref[0]

    @pl.when(j == 0)
    def _():
        m_s[...] = jnp.full(m_s.shape, NEG_FILL, jnp.float32)
        l_s[...] = jnp.zeros(l_s.shape, jnp.float32)
        acc_s[...] = jnp.zeros(acc_s.shape, jnp.float32)

    start = j * block

    def body(masked):
        ok = None
        if masked:
            cols = start + lax.broadcasted_iota(jnp.int32, (1, block), 1)
            ok = cols < n_valid
        for h in range(kv_heads):
            cols_h = slice(h * HD, (h + 1) * HD)
            m, l, acc = step(
                m_s[h], l_s[h], acc_s[h], q_ref[h], kv_ref[0, :, cols_h], kv_ref[1, :, cols_h],
                ones_ref[...], ok,
            )
            m_s[h] = m
            l_s[h] = l
            acc_s[h] = acc

    full = start + block <= n_valid
    part = jnp.logical_and(start < n_valid, jnp.logical_not(full))
    pl.when(full)(lambda: body(False))
    pl.when(part)(lambda: body(True))

    @pl.when(j == pl.num_programs(0) - 1)
    def _():
        m_out[...] = m_s[...]
        l_out[...] = l_s[...]
        acc_out[...] = acc_s[...]


def own_attend(q, kv, n_valid):
    kv_heads, rows, _ = q.shape
    cache_len = kv.shape[1]
    block = min(OWN_BLOCK, cache_len)
    n_blocks = cache_len // block

    def kv_map(j, nv):
        last = jnp.maximum((nv[0] + block - 1) // block - 1, 0)
        return (0, jnp.minimum(j, last), 0)

    state_shapes = (
        jax.ShapeDtypeStruct((kv_heads, rows, 1), jnp.float32),
        jax.ShapeDtypeStruct((kv_heads, rows, HD), jnp.float32),
        jax.ShapeDtypeStruct((kv_heads, rows, HD), jnp.float32),
    )
    ones = jnp.ones((block, HD), jnp.bfloat16)
    full3 = lambda j, nv: (0, 0, 0)
    return pl.pallas_call(
        functools.partial(own_kernel, kv_heads, block),
        out_shape=state_shapes,
        grid_spec=pltpu.PrefetchScalarGridSpec(
            num_scalar_prefetch=1,
            grid=(n_blocks,),
            in_specs=[
                pl.BlockSpec(q.shape, full3),
                pl.BlockSpec((2, block, kv.shape[2]), kv_map),
                pl.BlockSpec(ones.shape, lambda j, nv: (0, 0)),
            ],
            out_specs=[pl.BlockSpec(s.shape, full3) for s in state_shapes],
            scratch_shapes=[pltpu.VMEM(s.shape, jnp.float32) for s in state_shapes],
        ),
        compiler_params=pltpu.CompilerParams(dimension_semantics=("arbitrary",)),
        cost_estimate=pl.CostEstimate(
            flops=6 * kv_heads * rows * cache_len * HD,
            transcendentals=kv_heads * rows * cache_len,
            bytes_accessed=kv.size * 2 + q.size * 2,
        ),
    )(n_valid, q, kv, ones)


def shared_kernel(kv_heads, n_blocks, flag_ref, q_ref, m_ref, l_ref, acc_ref, *rest):
    blocks = rest[:n_blocks]
    dkv_ref, reach_ref, ones_ref, tree_ones_ref = rest[n_blocks:n_blocks + 4]
    m_out, l_out, acc_out = rest[n_blocks + 4:n_blocks + 7]
    for h in range(kv_heads):
        cols_h = slice(h * HD, (h + 1) * HD)
        q = q_ref[h]
        m, l, acc = m_ref[h], l_ref[h], acc_ref[h]
        for blk in blocks:
            m, l, acc = step(
                m, l, acc, q, blk[0, :, cols_h], blk[1, :, cols_h], ones_ref[...], None
            )
        m_out[h] = m
        l_out[h] = l
        acc_out[h] = acc

    @pl.when(flag_ref[0] == 1)
    def _():
        ok = reach_ref[...] > 0.5
        for h in range(kv_heads):
            cols_h = slice(h * HD, (h + 1) * HD)
            m, l, acc = step(
                m_out[h], l_out[h], acc_out[h], q_ref[h],
                dkv_ref[0, :, cols_h], dkv_ref[1, :, cols_h], tree_ones_ref[...], ok,
            )
            m_out[h] = m
            l_out[h] = l
            acc_out[h] = acc


def shared_attend(q, state, blocks, draft_kv, reach_rows, flag):
    kv_heads, rows, _ = q.shape
    n_blocks = len(blocks)
    whole = lambda a: pl.BlockSpec(a.shape, lambda i, f: (0,) * a.ndim)
    ones = jnp.ones((blocks[0].shape[1], HD), jnp.bfloat16)
    tree_ones = jnp.ones((draft_kv.shape[1], HD), jnp.bfloat16)
    operands = (q,) + tuple(state) + tuple(blocks) + (draft_kv, reach_rows, ones, tree_ones)
    keys = sum(b.shape[1] for b in blocks)
    return pl.pallas_call(
        functools.partial(shared_kernel, kv_heads, n_blocks),
        out_shape=tuple(jax.ShapeDtypeStruct(s.shape, s.dtype) for s in state),
        grid_spec=pltpu.PrefetchScalarGridSpec(
            num_scalar_prefetch=1,
            grid=(1,),
            in_specs=[whole(a) for a in operands],
            out_specs=[whole(s) for s in state],
        ),
        compiler_params=pltpu.CompilerParams(vmem_limit_bytes=48 * 1024 * 1024),
        cost_estimate=pl.CostEstimate(
            flops=6 * kv_heads * rows * keys * HD,
            transcendentals=kv_heads * rows * keys,
            bytes_accessed=sum(b.size * 2 for b in blocks) + q.size * 2,
        ),
    )(flag, *operands)


def tree_reach(parent_row):
    node_count = parent_row.shape[0]
    nodes = jnp.arange(node_count, dtype=jnp.int32)
    reach = jnp.eye(node_count, dtype=jnp.float32) + (parent_row[:, None] == nodes[None, :]).astype(
        jnp.float32
    )
    for level_step in range(max(node_count - 1, 1).bit_length()):
        reach = jnp.minimum(jnp.dot(reach, reach, precision=lax.Precision.HIGHEST), 1.0)
    return reach > 0.5


def exchange_shared(shared_cache, group_ids, req_index, req_count):
    local = shared_cache[:, group_ids[req_index]]
    received = [local]
    pow2 = req_count & (req_count - 1) == 0
    for k in range(1, req_count):
        if pow2:
            pairs = [(r, r ^ k) for r in range(req_count)]
            dst = req_index ^ k
        else:
            pairs = [(r, (r + k) % req_count) for r in range(req_count)]
            dst = (req_index + k) % req_count
        sent = lax.dynamic_index_in_dim(shared_cache, group_ids[dst], 1, keepdims=False)
        received.append(lax.ppermute(sent, "req", pairs))
    return received


def shards(
    draft_query,
    draft_kv,
    own_cache,
    shared_cache,
    out_weight,
    lengths,
    group_ids,
    parents,
    accepted,
):
    kv_heads = own_cache.shape[3] // HD
    draft_len = draft_query.shape[1]
    rows = QPK * draft_len
    seq_count = lax.axis_size("seq")
    seq_index = lax.axis_index("seq")
    req_index = lax.axis_index("req")
    req_count = lax.axis_size("req")
    cache_len = own_cache.shape[2]

    blocks = exchange_shared(shared_cache, group_ids, req_index, req_count)

    queries = (
        draft_query[0]
        .reshape(draft_len, kv_heads, QPK, HD)
        .transpose(1, 2, 0, 3)
        .reshape(kv_heads, rows, HD)
    )
    n_valid = jnp.clip(lengths[0] - seq_index * cache_len, 0, cache_len).astype(jnp.int32)
    state = own_attend(queries, own_cache[0], n_valid.reshape(1))

    reach = tree_reach(parents[0])
    reach_rows = jnp.tile(reach.astype(jnp.float32), (QPK, 1))
    flag = (seq_index == 0).astype(jnp.int32).reshape(1)
    m, l, acc = shared_attend(queries, state, blocks, draft_kv[0], reach_rows, flag)

    heads_dev = kv_heads * QPK
    share = heads_dev // seq_count
    stats = jnp.concatenate(
        [m[..., 0].reshape(heads_dev, draft_len), l[..., 0].reshape(heads_dev, draft_len)], 1
    )
    packed = jnp.concatenate(
        [acc.reshape(heads_dev, draft_len, HD), stats.reshape(heads_dev, 1, 2 * draft_len)], 1
    )
    packed = lax.all_to_all(packed, "seq", 0, 0, tiled=True)
    packed = packed.reshape(seq_count, share, draft_len + 1, 2 * draft_len)
    part_max = packed[:, :, draft_len, :draft_len]
    part_total = packed[:, :, draft_len, draft_len:]
    part_sum = packed[:, :, :draft_len, :]
    final_max = jnp.max(part_max, axis=0)
    factor = jnp.exp2((part_max - final_max[None]) * EXP2_SCALE)
    final_total = jnp.sum(part_total * factor, axis=0)
    final_sum = jnp.sum(part_sum * factor[..., None], axis=0)
    attended = (final_sum / final_total[..., None]).astype(jnp.bfloat16)
    attended = jnp.transpose(attended, (1, 0, 2)).reshape(draft_len, share * HD)
    out_piece = lax.psum_scatter(
        lax.dot_general(
            out_weight, attended, (((0,), (1,)), ((), ())), preferred_element_type=jnp.float32
        ).astype(jnp.bfloat16),
        ("tensor", "seq"),
        scatter_dimension=0,
        tiled=True,
    )
    verified = out_piece.T[None]
    accepted_kv = jnp.take(draft_kv[0], accepted[0], axis=1)[None]
    return (verified, accepted_kv)


def solution(mesh):
    placed = (
        P("req", None, "tensor"),
        P("req", None, None, "tensor"),
        P("req", None, "seq", "tensor"),
        P(None, None, ("req", "seq"), "tensor"),
        P(("tensor", "seq"), None),
        P("req"),
        P(),
        P("req", None),
        P("req", None),
    )
    return jax.shard_map(
        shards,
        mesh=mesh,
        in_specs=placed,
        out_specs=(P("req", None, ("tensor", "seq")), P("req", None, None, "tensor")),
        check_vma=False,
    )
```

```python
import functools

import jax
import jax.numpy as jnp
from jax import lax
from jax.experimental import pallas as pl
from jax.experimental.pallas import tpu as pltpu
from jax.sharding import PartitionSpec as P

HD = 128
QPK = 8
NEG_FILL = -1e30
SCALE = HD ** (-0.5)
EXP2_SCALE = SCALE * 1.4426950408889634
OWN_BLOCK = 512


def step(m_prev, l_prev, acc_prev, q, k, v, ones, ok):
    scores = lax.dot_general(
        q, k, (((1,), (1,)), ((), ())), preferred_element_type=jnp.float32
    )
    if ok is not None:
        scores = jnp.where(ok, scores, NEG_FILL)
    m_new = jnp.maximum(m_prev, jnp.max(scores, axis=1, keepdims=True))
    alpha = jnp.exp2((m_prev - m_new) * EXP2_SCALE)
    weights = jnp.exp2((scores - m_new) * EXP2_SCALE)
    if ok is not None:
        weights = jnp.where(ok, weights, 0.0)
    weights = weights.astype(jnp.bfloat16)
    l_new = alpha * l_prev + jnp.dot(weights, ones, preferred_element_type=jnp.float32)
    acc_new = alpha * acc_prev + jnp.dot(weights, v, preferred_element_type=jnp.float32)
    return m_new, l_new, acc_new


def own_kernel(kv_heads, block, nv_ref, q_ref, kv_ref, ones_ref, m_out, l_out, acc_out, m_s, l_s, acc_s):
    j = pl.program_id(0)
    n_valid = nv_ref[0]

    @pl.when(j == 0)
    def _():
        m_s[...] = jnp.full(m_s.shape, NEG_FILL, jnp.float32)
        l_s[...] = jnp.zeros(l_s.shape, jnp.float32)
        acc_s[...] = jnp.zeros(acc_s.shape, jnp.float32)

    start = j * block

    def body(masked):
        ok = None
        if masked:
            cols = start + lax.broadcasted_iota(jnp.int32, (1, block), 1)
            ok = cols < n_valid
        for h in range(kv_heads):
            cols_h = slice(h * HD, (h + 1) * HD)
            m, l, acc = step(
                m_s[h], l_s[h], acc_s[h], q_ref[h], kv_ref[0, :, cols_h], kv_ref[1, :, cols_h],
                ones_ref[...], ok,
            )
            m_s[h] = m
            l_s[h] = l
            acc_s[h] = acc

    full = start + block <= n_valid
    part = jnp.logical_and(start < n_valid, jnp.logical_not(full))
    pl.when(full)(lambda: body(False))
    pl.when(part)(lambda: body(True))

    @pl.when(j == pl.num_programs(0) - 1)
    def _():
        m_out[...] = m_s[...]
        l_out[...] = l_s[...]
        acc_out[...] = acc_s[...]


def own_attend(q, kv, n_valid):
    kv_heads, rows, _ = q.shape
    cache_len = kv.shape[1]
    block = min(OWN_BLOCK, cache_len)
    n_blocks = cache_len // block

    def kv_map(j, nv):
        last = jnp.maximum((nv[0] + block - 1) // block - 1, 0)
        return (0, jnp.minimum(j, last), 0)

    state_shapes = (
        jax.ShapeDtypeStruct((kv_heads, rows, 1), jnp.float32),
        jax.ShapeDtypeStruct((kv_heads, rows, HD), jnp.float32),
        jax.ShapeDtypeStruct((kv_heads, rows, HD), jnp.float32),
    )
    ones = jnp.ones((block, HD), jnp.bfloat16)
    full3 = lambda j, nv: (0, 0, 0)
    return pl.pallas_call(
        functools.partial(own_kernel, kv_heads, block),
        out_shape=state_shapes,
        grid_spec=pltpu.PrefetchScalarGridSpec(
            num_scalar_prefetch=1,
            grid=(n_blocks,),
            in_specs=[
                pl.BlockSpec(q.shape, full3),
                pl.BlockSpec((2, block, kv.shape[2]), kv_map),
                pl.BlockSpec(ones.shape, lambda j, nv: (0, 0)),
            ],
            out_specs=[pl.BlockSpec(s.shape, full3) for s in state_shapes],
            scratch_shapes=[pltpu.VMEM(s.shape, jnp.float32) for s in state_shapes],
        ),
        compiler_params=pltpu.CompilerParams(dimension_semantics=("arbitrary",)),
        cost_estimate=pl.CostEstimate(
            flops=6 * kv_heads * rows * cache_len * HD,
            transcendentals=kv_heads * rows * cache_len,
            bytes_accessed=kv.size * 2 + q.size * 2,
        ),
    )(n_valid, q, kv, ones)


def shared_kernel(kv_heads, n_blocks, with_tree, flag_ref, q_ref, m_ref, l_ref, acc_ref, *rest):
    blocks = rest[:n_blocks]
    ones_ref = rest[n_blocks]
    rest = rest[n_blocks + 1:]
    if with_tree:
        dkv_ref, reach_ref, tree_ones_ref = rest[:3]
        rest = rest[3:]
    m_out, l_out, acc_out = rest[:3]
    for h in range(kv_heads):
        cols_h = slice(h * HD, (h + 1) * HD)
        q = q_ref[h]
        m, l, acc = m_ref[h], l_ref[h], acc_ref[h]
        for blk in blocks:
            m, l, acc = step(
                m, l, acc, q, blk[0, :, cols_h], blk[1, :, cols_h], ones_ref[...], None
            )
        m_out[h] = m
        l_out[h] = l
        acc_out[h] = acc

    if with_tree:
        @pl.when(flag_ref[0] == 1)
        def _():
            ok = reach_ref[...] > 0.5
            for h in range(kv_heads):
                cols_h = slice(h * HD, (h + 1) * HD)
                m, l, acc = step(
                    m_out[h], l_out[h], acc_out[h], q_ref[h],
                    dkv_ref[0, :, cols_h], dkv_ref[1, :, cols_h], tree_ones_ref[...], ok,
                )
                m_out[h] = m
                l_out[h] = l
                acc_out[h] = acc


def shared_attend(q, state, blocks, tree=None):
    kv_heads, rows, _ = q.shape
    n_blocks = len(blocks)
    whole = lambda a: pl.BlockSpec(a.shape, lambda i, f: (0,) * a.ndim)
    ones = jnp.ones((blocks[0].shape[1], HD), jnp.bfloat16)
    operands = (q,) + tuple(state) + tuple(blocks) + (ones,)
    if tree is not None:
        draft_kv, reach_rows, flag = tree
        operands += (draft_kv, reach_rows, jnp.ones((draft_kv.shape[1], HD), jnp.bfloat16))
    else:
        flag = jnp.zeros((1,), jnp.int32)
    keys = sum(b.shape[1] for b in blocks)
    return pl.pallas_call(
        functools.partial(shared_kernel, kv_heads, n_blocks, tree is not None),
        out_shape=tuple(jax.ShapeDtypeStruct(s.shape, s.dtype) for s in state),
        grid_spec=pltpu.PrefetchScalarGridSpec(
            num_scalar_prefetch=1,
            grid=(1,),
            in_specs=[whole(a) for a in operands],
            out_specs=[whole(s) for s in state],
        ),
        compiler_params=pltpu.CompilerParams(vmem_limit_bytes=48 * 1024 * 1024),
        cost_estimate=pl.CostEstimate(
            flops=6 * kv_heads * rows * keys * HD,
            transcendentals=kv_heads * rows * keys,
            bytes_accessed=sum(b.size * 2 for b in blocks) + q.size * 2,
        ),
    )(flag, *operands)


def tree_reach(parent_row):
    node_count = parent_row.shape[0]
    nodes = jnp.arange(node_count, dtype=jnp.int32)
    reach = jnp.eye(node_count, dtype=jnp.float32) + (parent_row[:, None] == nodes[None, :]).astype(
        jnp.float32
    )
    for level_step in range(max(node_count - 1, 1).bit_length()):
        reach = jnp.minimum(jnp.dot(reach, reach, precision=lax.Precision.HIGHEST), 1.0)
    return reach > 0.5


def exchange_shared(shared_cache, group_ids, req_index, req_count):
    local = shared_cache[:, group_ids[req_index]]
    received = [local]
    pow2 = req_count & (req_count - 1) == 0
    for k in range(1, req_count):
        if pow2:
            pairs = [(r, r ^ k) for r in range(req_count)]
            dst = req_index ^ k
        else:
            pairs = [(r, (r + k) % req_count) for r in range(req_count)]
            dst = (req_index + k) % req_count
        sent = lax.dynamic_index_in_dim(shared_cache, group_ids[dst], 1, keepdims=False)
        received.append(lax.ppermute(sent, "req", pairs))
    return received


def shards(
    draft_query,
    draft_kv,
    own_cache,
    shared_cache,
    out_weight,
    lengths,
    group_ids,
    parents,
    accepted,
):
    kv_heads = own_cache.shape[3] // HD
    draft_len = draft_query.shape[1]
    rows = QPK * draft_len
    seq_count = lax.axis_size("seq")
    seq_index = lax.axis_index("seq")
    req_index = lax.axis_index("req")
    req_count = lax.axis_size("req")
    cache_len = own_cache.shape[2]

    blocks = exchange_shared(shared_cache, group_ids, req_index, req_count)

    queries = (
        draft_query[0]
        .reshape(draft_len, kv_heads, QPK, HD)
        .transpose(1, 2, 0, 3)
        .reshape(kv_heads, rows, HD)
    )
    n_valid = jnp.clip(lengths[0] - seq_index * cache_len, 0, cache_len).astype(jnp.int32)
    state = own_attend(queries, own_cache[0], n_valid.reshape(1))

    reach = tree_reach(parents[0])
    reach_rows = jnp.tile(reach.astype(jnp.float32), (QPK, 1))
    flag = (seq_index == 0).astype(jnp.int32).reshape(1)
    state = shared_attend(queries, state, blocks[:1], (draft_kv[0], reach_rows, flag))
    for blk in blocks[1:]:
        state = shared_attend(queries, state, [blk])
    m, l, acc = state

    heads_dev = kv_heads * QPK
    share = heads_dev // seq_count
    stats = jnp.concatenate(
        [m[..., 0].reshape(heads_dev, draft_len), l[..., 0].reshape(heads_dev, draft_len)], 1
    )
    packed = jnp.concatenate(
        [acc.reshape(heads_dev, draft_len, HD), stats.reshape(heads_dev, 1, 2 * draft_len)], 1
    )
    packed = lax.all_to_all(packed, "seq", 0, 0, tiled=True)
    packed = packed.reshape(seq_count, share, draft_len + 1, 2 * draft_len)
    part_max = packed[:, :, draft_len, :draft_len]
    part_total = packed[:, :, draft_len, draft_len:]
    part_sum = packed[:, :, :draft_len, :]
    final_max = jnp.max(part_max, axis=0)
    factor = jnp.exp2((part_max - final_max[None]) * EXP2_SCALE)
    final_total = jnp.sum(part_total * factor, axis=0)
    final_sum = jnp.sum(part_sum * factor[..., None], axis=0)
    attended = (final_sum / final_total[..., None]).astype(jnp.bfloat16)
    attended = jnp.transpose(attended, (1, 0, 2)).reshape(draft_len, share * HD)
    out_piece = lax.psum_scatter(
        lax.dot_general(
            out_weight, attended, (((0,), (1,)), ((), ())), preferred_element_type=jnp.float32
        ).astype(jnp.bfloat16),
        ("tensor", "seq"),
        scatter_dimension=0,
        tiled=True,
    )
    verified = out_piece.T[None]
    accepted_kv = jnp.take(draft_kv[0], accepted[0], axis=1)[None]
    return (verified, accepted_kv)


def solution(mesh):
    placed = (
        P("req", None, "tensor"),
        P("req", None, None, "tensor"),
        P("req", None, "seq", "tensor"),
        P(None, None, ("req", "seq"), "tensor"),
        P(("tensor", "seq"), None),
        P("req"),
        P(),
        P("req", None),
        P("req", None),
    )
    return jax.shard_map(
        shards,
        mesh=mesh,
        in_specs=placed,
        out_specs=(P("req", None, ("tensor", "seq")), P("req", None, None, "tensor")),
        check_vma=False,
    )
```

```python
import functools

import jax
import jax.numpy as jnp
from jax import lax
from jax.experimental import pallas as pl
from jax.experimental.pallas import tpu as pltpu
from jax.sharding import PartitionSpec as P

HD = 128
QPK = 8
NEG_FILL = -1e30
SCALE = HD ** (-0.5)
EXP2_SCALE = SCALE * 1.4426950408889634
OWN_BLOCK = 512


def step(m_prev, l_prev, acc_prev, q, k, v, ones, ok):
    scores = lax.dot_general(
        q, k, (((1,), (1,)), ((), ())), preferred_element_type=jnp.float32
    )
    if ok is not None:
        scores = jnp.where(ok, scores, NEG_FILL)
    m_new = jnp.maximum(m_prev, jnp.max(scores, axis=1, keepdims=True))
    alpha = jnp.exp2((m_prev - m_new) * EXP2_SCALE)
    weights = jnp.exp2((scores - m_new) * EXP2_SCALE)
    if ok is not None:
        weights = jnp.where(ok, weights, 0.0)
    weights = weights.astype(jnp.bfloat16)
    l_new = alpha * l_prev + jnp.dot(weights, ones, preferred_element_type=jnp.float32)
    acc_new = alpha * acc_prev + jnp.dot(weights, v, preferred_element_type=jnp.float32)
    return m_new, l_new, acc_new


def own_kernel(kv_heads, block, nv_ref, q_ref, kv_ref, ones_ref, m_out, l_out, acc_out, m_s, l_s, acc_s):
    j = pl.program_id(0)
    n_valid = nv_ref[0]

    @pl.when(j == 0)
    def _():
        m_s[...] = jnp.full(m_s.shape, NEG_FILL, jnp.float32)
        l_s[...] = jnp.zeros(l_s.shape, jnp.float32)
        acc_s[...] = jnp.zeros(acc_s.shape, jnp.float32)

    start = j * block

    def body(masked):
        ok = None
        if masked:
            cols = start + lax.broadcasted_iota(jnp.int32, (1, block), 1)
            ok = cols < n_valid
        for h in range(kv_heads):
            cols_h = slice(h * HD, (h + 1) * HD)
            m, l, acc = step(
                m_s[h], l_s[h], acc_s[h], q_ref[h], kv_ref[0, :, cols_h], kv_ref[1, :, cols_h],
                ones_ref[...], ok,
            )
            m_s[h] = m
            l_s[h] = l
            acc_s[h] = acc

    full = start + block <= n_valid
    part = jnp.logical_and(start < n_valid, jnp.logical_not(full))
    pl.when(full)(lambda: body(False))
    pl.when(part)(lambda: body(True))

    @pl.when(j == pl.num_programs(0) - 1)
    def _():
        m_out[...] = m_s[...]
        l_out[...] = l_s[...]
        acc_out[...] = acc_s[...]


def own_attend(q, kv, n_valid):
    kv_heads, rows, _ = q.shape
    cache_len = kv.shape[1]
    block = min(OWN_BLOCK, cache_len)
    n_blocks = cache_len // block

    def kv_map(j, nv):
        last = jnp.maximum((nv[0] + block - 1) // block - 1, 0)
        return (0, jnp.minimum(j, last), 0)

    state_shapes = (
        jax.ShapeDtypeStruct((kv_heads, rows, 1), jnp.float32),
        jax.ShapeDtypeStruct((kv_heads, rows, HD), jnp.float32),
        jax.ShapeDtypeStruct((kv_heads, rows, HD), jnp.float32),
    )
    ones = jnp.ones((block, HD), jnp.bfloat16)
    full3 = lambda j, nv: (0, 0, 0)
    return pl.pallas_call(
        functools.partial(own_kernel, kv_heads, block),
        out_shape=state_shapes,
        grid_spec=pltpu.PrefetchScalarGridSpec(
            num_scalar_prefetch=1,
            grid=(n_blocks,),
            in_specs=[
                pl.BlockSpec(q.shape, full3),
                pl.BlockSpec((2, block, kv.shape[2]), kv_map),
                pl.BlockSpec(ones.shape, lambda j, nv: (0, 0)),
            ],
            out_specs=[pl.BlockSpec(s.shape, full3) for s in state_shapes],
            scratch_shapes=[pltpu.VMEM(s.shape, jnp.float32) for s in state_shapes],
        ),
        compiler_params=pltpu.CompilerParams(dimension_semantics=("arbitrary",)),
        cost_estimate=pl.CostEstimate(
            flops=6 * kv_heads * rows * cache_len * HD,
            transcendentals=kv_heads * rows * cache_len,
            bytes_accessed=kv.size * 2 + q.size * 2,
        ),
    )(n_valid, q, kv, ones)


def shared_kernel(kv_heads, n_blocks, with_tree, flag_ref, q_ref, m_ref, l_ref, acc_ref, *rest):
    blocks = rest[:n_blocks]
    ones_ref = rest[n_blocks]
    rest = rest[n_blocks + 1:]
    if with_tree:
        dkv_ref, reach_ref, tree_ones_ref = rest[:3]
        rest = rest[3:]
    m_out, l_out, acc_out = rest[:3]
    for h in range(kv_heads):
        cols_h = slice(h * HD, (h + 1) * HD)
        q = q_ref[h]
        m, l, acc = m_ref[h], l_ref[h], acc_ref[h]
        for blk in blocks:
            m, l, acc = step(
                m, l, acc, q, blk[0, :, cols_h], blk[1, :, cols_h], ones_ref[...], None
            )
        m_out[h] = m
        l_out[h] = l
        acc_out[h] = acc

    if with_tree:
        @pl.when(flag_ref[0] == 1)
        def _():
            ok = reach_ref[...] > 0.5
            for h in range(kv_heads):
                cols_h = slice(h * HD, (h + 1) * HD)
                m, l, acc = step(
                    m_out[h], l_out[h], acc_out[h], q_ref[h],
                    dkv_ref[0, :, cols_h], dkv_ref[1, :, cols_h], tree_ones_ref[...], ok,
                )
                m_out[h] = m
                l_out[h] = l
                acc_out[h] = acc


def shared_attend(q, state, blocks, tree=None):
    kv_heads, rows, _ = q.shape
    n_blocks = len(blocks)
    whole = lambda a: pl.BlockSpec(a.shape, lambda i, f: (0,) * a.ndim)
    ones = jnp.ones((blocks[0].shape[1], HD), jnp.bfloat16)
    operands = (q,) + tuple(state) + tuple(blocks) + (ones,)
    if tree is not None:
        draft_kv, reach_rows, flag = tree
        operands += (draft_kv, reach_rows, jnp.ones((draft_kv.shape[1], HD), jnp.bfloat16))
    else:
        flag = jnp.zeros((1,), jnp.int32)
    keys = sum(b.shape[1] for b in blocks)
    return pl.pallas_call(
        functools.partial(shared_kernel, kv_heads, n_blocks, tree is not None),
        out_shape=tuple(jax.ShapeDtypeStruct(s.shape, s.dtype) for s in state),
        grid_spec=pltpu.PrefetchScalarGridSpec(
            num_scalar_prefetch=1,
            grid=(1,),
            in_specs=[whole(a) for a in operands],
            out_specs=[whole(s) for s in state],
        ),
        compiler_params=pltpu.CompilerParams(vmem_limit_bytes=48 * 1024 * 1024),
        cost_estimate=pl.CostEstimate(
            flops=6 * kv_heads * rows * keys * HD,
            transcendentals=kv_heads * rows * keys,
            bytes_accessed=sum(b.size * 2 for b in blocks) + q.size * 2,
        ),
    )(flag, *operands)


def tree_reach(parent_row):
    node_count = parent_row.shape[0]
    nodes = jnp.arange(node_count, dtype=jnp.int32)
    reach = jnp.eye(node_count, dtype=jnp.float32) + (parent_row[:, None] == nodes[None, :]).astype(
        jnp.float32
    )
    for level_step in range(max(node_count - 1, 1).bit_length()):
        reach = jnp.minimum(jnp.dot(reach, reach, precision=lax.Precision.HIGHEST), 1.0)
    return reach > 0.5


def exchange_shared(shared_cache, group_ids, req_index, req_count):
    local = shared_cache[:, group_ids[req_index]]
    received = [local]
    pow2 = req_count & (req_count - 1) == 0
    for k in range(1, req_count):
        if pow2:
            pairs = [(r, r ^ k) for r in range(req_count)]
            dst = req_index ^ k
        else:
            pairs = [(r, (r + k) % req_count) for r in range(req_count)]
            dst = (req_index + k) % req_count
        sent = lax.dynamic_index_in_dim(shared_cache, group_ids[dst], 1, keepdims=False)
        received.append(lax.ppermute(sent, "req", pairs))
    return received


def shards(
    draft_query,
    draft_kv,
    own_cache,
    shared_cache,
    out_weight,
    lengths,
    group_ids,
    parents,
    accepted,
):
    kv_heads = own_cache.shape[3] // HD
    draft_len = draft_query.shape[1]
    rows = QPK * draft_len
    seq_count = lax.axis_size("seq")
    seq_index = lax.axis_index("seq")
    req_index = lax.axis_index("req")
    req_count = lax.axis_size("req")
    cache_len = own_cache.shape[2]

    blocks = exchange_shared(shared_cache, group_ids, req_index, req_count)

    queries = (
        draft_query[0]
        .reshape(draft_len, kv_heads, QPK, HD)
        .transpose(1, 2, 0, 3)
        .reshape(kv_heads, rows, HD)
    )
    n_valid = jnp.clip(lengths[0] - seq_index * cache_len, 0, cache_len).astype(jnp.int32)
    state = own_attend(queries, own_cache[0], n_valid.reshape(1))

    reach = tree_reach(parents[0])
    reach_rows = jnp.tile(reach.astype(jnp.float32), (QPK, 1))
    flag = (seq_index == 0).astype(jnp.int32).reshape(1)
    state = shared_attend(queries, state, blocks[:1], (draft_kv[0], reach_rows, flag))
    for blk in blocks[1:]:
        state = shared_attend(queries, state, [blk])
    m, l, acc = state

    heads_dev = kv_heads * QPK
    share = heads_dev // seq_count
    stats = jnp.concatenate(
        [m[..., 0].reshape(heads_dev, draft_len), l[..., 0].reshape(heads_dev, draft_len)], 1
    )
    packed = jnp.concatenate(
        [acc.reshape(heads_dev, draft_len, HD), stats.reshape(heads_dev, 1, 2 * draft_len)], 1
    )
    packed = lax.all_to_all(packed, "seq", 0, 0, tiled=True)
    packed = packed.reshape(seq_count, share, draft_len + 1, 2 * draft_len)
    part_max = packed[:, :, draft_len, :draft_len]
    part_total = packed[:, :, draft_len, draft_len:]
    part_sum = packed[:, :, :draft_len, :]
    final_max = jnp.max(part_max, axis=0)
    factor = jnp.exp2((part_max - final_max[None]) * EXP2_SCALE)
    final_total = jnp.sum(part_total * factor, axis=0)
    final_sum = jnp.sum(part_sum * factor[..., None], axis=0)
    attended = (final_sum / final_total[..., None]).astype(jnp.bfloat16)
    attended = jnp.transpose(attended, (1, 0, 2)).reshape(draft_len, share * HD)
    out_group = ("tensor", "seq")
    owners = lax.axis_size("tensor") * seq_count
    columns = out_weight.shape[1] // owners
    product = jnp.einsum(
        "ik,kcj->cij",
        attended,
        out_weight.reshape(out_weight.shape[0], owners, columns),
        preferred_element_type=jnp.float32,
    ).astype(jnp.bfloat16)
    pieces = lax.all_to_all(product, out_group, 0, 0, tiled=True)
    verified = jnp.sum(pieces.astype(jnp.float32), axis=0).astype(jnp.bfloat16)[None]
    accepted_kv = jnp.take(draft_kv[0], accepted[0], axis=1)[None]
    return (verified, accepted_kv)


def solution(mesh):
    placed = (
        P("req", None, "tensor"),
        P("req", None, None, "tensor"),
        P("req", None, "seq", "tensor"),
        P(None, None, ("req", "seq"), "tensor"),
        P(("tensor", "seq"), None),
        P("req"),
        P(),
        P("req", None),
        P("req", None),
    )
    return jax.shard_map(
        shards,
        mesh=mesh,
        in_specs=placed,
        out_specs=(P("req", None, ("tensor", "seq")), P("req", None, None, "tensor")),
        check_vma=False,
    )
```

```python
import functools

import jax
import jax.numpy as jnp
from jax import lax
from jax.experimental import pallas as pl
from jax.experimental.pallas import tpu as pltpu
from jax.sharding import PartitionSpec as P

HD = 128
QPK = 8
NEG_FILL = -1e30
SCALE = HD ** (-0.5)
EXP2_SCALE = SCALE * 1.4426950408889634
OWN_BLOCK = 512


def step(m_prev, l_prev, acc_prev, q, k, v, ones, ok):
    scores = lax.dot_general(
        q, k, (((1,), (1,)), ((), ())), preferred_element_type=jnp.float32
    )
    if ok is not None:
        scores = jnp.where(ok, scores, NEG_FILL)
    m_new = jnp.maximum(m_prev, jnp.max(scores, axis=1, keepdims=True))
    alpha = jnp.exp2((m_prev - m_new) * EXP2_SCALE)
    weights = jnp.exp2((scores - m_new) * EXP2_SCALE)
    if ok is not None:
        weights = jnp.where(ok, weights, 0.0)
    weights = weights.astype(jnp.bfloat16)
    l_new = alpha * l_prev + jnp.dot(weights, ones, preferred_element_type=jnp.float32)
    acc_new = alpha * acc_prev + jnp.dot(weights, v, preferred_element_type=jnp.float32)
    return m_new, l_new, acc_new


def own_kernel(kv_heads, block, nv_ref, q_ref, kv_ref, ones_ref, m_out, l_out, acc_out, m_s, l_s, acc_s):
    j = pl.program_id(0)
    n_valid = nv_ref[0]

    @pl.when(j == 0)
    def _():
        m_s[...] = jnp.full(m_s.shape, NEG_FILL, jnp.float32)
        l_s[...] = jnp.zeros(l_s.shape, jnp.float32)
        acc_s[...] = jnp.zeros(acc_s.shape, jnp.float32)

    start = j * block

    def body(masked):
        ok = None
        if masked:
            cols = start + lax.broadcasted_iota(jnp.int32, (1, block), 1)
            ok = cols < n_valid
        for h in range(kv_heads):
            cols_h = slice(h * HD, (h + 1) * HD)
            m, l, acc = step(
                m_s[h], l_s[h], acc_s[h], q_ref[h], kv_ref[0, :, cols_h], kv_ref[1, :, cols_h],
                ones_ref[...], ok,
            )
            m_s[h] = m
            l_s[h] = l
            acc_s[h] = acc

    full = start + block <= n_valid
    part = jnp.logical_and(start < n_valid, jnp.logical_not(full))
    pl.when(full)(lambda: body(False))
    pl.when(part)(lambda: body(True))

    @pl.when(j == pl.num_programs(0) - 1)
    def _():
        m_out[...] = m_s[...]
        l_out[...] = l_s[...]
        acc_out[...] = acc_s[...]


def own_attend(q, kv, n_valid):
    kv_heads, rows, _ = q.shape
    cache_len = kv.shape[1]
    block = min(OWN_BLOCK, cache_len)
    n_blocks = cache_len // block

    def kv_map(j, nv):
        last = jnp.maximum((nv[0] + block - 1) // block - 1, 0)
        return (0, jnp.minimum(j, last), 0)

    state_shapes = (
        jax.ShapeDtypeStruct((kv_heads, rows, 1), jnp.float32),
        jax.ShapeDtypeStruct((kv_heads, rows, HD), jnp.float32),
        jax.ShapeDtypeStruct((kv_heads, rows, HD), jnp.float32),
    )
    ones = jnp.ones((block, HD), jnp.bfloat16)
    full3 = lambda j, nv: (0, 0, 0)
    return pl.pallas_call(
        functools.partial(own_kernel, kv_heads, block),
        out_shape=state_shapes,
        grid_spec=pltpu.PrefetchScalarGridSpec(
            num_scalar_prefetch=1,
            grid=(n_blocks,),
            in_specs=[
                pl.BlockSpec(q.shape, full3),
                pl.BlockSpec((2, block, kv.shape[2]), kv_map),
                pl.BlockSpec(ones.shape, lambda j, nv: (0, 0)),
            ],
            out_specs=[pl.BlockSpec(s.shape, full3) for s in state_shapes],
            scratch_shapes=[pltpu.VMEM(s.shape, jnp.float32) for s in state_shapes],
        ),
        compiler_params=pltpu.CompilerParams(dimension_semantics=("arbitrary",)),
        cost_estimate=pl.CostEstimate(
            flops=6 * kv_heads * rows * cache_len * HD,
            transcendentals=kv_heads * rows * cache_len,
            bytes_accessed=kv.size * 2 + q.size * 2,
        ),
    )(n_valid, q, kv, ones)


def shared_kernel(kv_heads, n_blocks, with_tree, flag_ref, q_ref, m_ref, l_ref, acc_ref, *rest):
    blocks = rest[:n_blocks]
    ones_ref = rest[n_blocks]
    rest = rest[n_blocks + 1:]
    if with_tree:
        dkv_ref, reach_ref, tree_ones_ref = rest[:3]
        rest = rest[3:]
    m_out, l_out, acc_out = rest[:3]
    for h in range(kv_heads):
        cols_h = slice(h * HD, (h + 1) * HD)
        q = q_ref[h]
        m, l, acc = m_ref[h], l_ref[h], acc_ref[h]
        for blk in blocks:
            m, l, acc = step(
                m, l, acc, q, blk[0, :, cols_h], blk[1, :, cols_h], ones_ref[...], None
            )
        m_out[h] = m
        l_out[h] = l
        acc_out[h] = acc

    if with_tree:
        @pl.when(flag_ref[0] == 1)
        def _():
            ok = reach_ref[...] > 0.5
            for h in range(kv_heads):
                cols_h = slice(h * HD, (h + 1) * HD)
                m, l, acc = step(
                    m_out[h], l_out[h], acc_out[h], q_ref[h],
                    dkv_ref[0, :, cols_h], dkv_ref[1, :, cols_h], tree_ones_ref[...], ok,
                )
                m_out[h] = m
                l_out[h] = l
                acc_out[h] = acc


def shared_attend(q, state, blocks, tree=None):
    kv_heads, rows, _ = q.shape
    n_blocks = len(blocks)
    whole = lambda a: pl.BlockSpec(a.shape, lambda i, f: (0,) * a.ndim)
    ones = jnp.ones((blocks[0].shape[1], HD), jnp.bfloat16)
    operands = (q,) + tuple(state) + tuple(blocks) + (ones,)
    if tree is not None:
        draft_kv, reach_rows, flag = tree
        operands += (draft_kv, reach_rows, jnp.ones((draft_kv.shape[1], HD), jnp.bfloat16))
    else:
        flag = jnp.zeros((1,), jnp.int32)
    keys = sum(b.shape[1] for b in blocks)
    return pl.pallas_call(
        functools.partial(shared_kernel, kv_heads, n_blocks, tree is not None),
        out_shape=tuple(jax.ShapeDtypeStruct(s.shape, s.dtype) for s in state),
        grid_spec=pltpu.PrefetchScalarGridSpec(
            num_scalar_prefetch=1,
            grid=(1,),
            in_specs=[whole(a) for a in operands],
            out_specs=[whole(s) for s in state],
        ),
        compiler_params=pltpu.CompilerParams(vmem_limit_bytes=48 * 1024 * 1024),
        cost_estimate=pl.CostEstimate(
            flops=6 * kv_heads * rows * keys * HD,
            transcendentals=kv_heads * rows * keys,
            bytes_accessed=sum(b.size * 2 for b in blocks) + q.size * 2,
        ),
    )(flag, *operands)


def tree_reach(parent_row):
    node_count = parent_row.shape[0]
    nodes = jnp.arange(node_count, dtype=jnp.int32)
    reach = jnp.eye(node_count, dtype=jnp.float32) + (parent_row[:, None] == nodes[None, :]).astype(
        jnp.float32
    )
    for level_step in range(max(node_count - 1, 1).bit_length()):
        reach = jnp.minimum(jnp.dot(reach, reach, precision=lax.Precision.HIGHEST), 1.0)
    return reach > 0.5


def pick_group(shared_cache, group_ids, request):
    onehot = jnp.arange(group_ids.shape[0], dtype=jnp.int32) == request
    group = jnp.sum(jnp.where(onehot, group_ids, 0))
    picked = shared_cache[:, 0]
    for g in range(1, shared_cache.shape[1]):
        picked = jnp.where(group == g, shared_cache[:, g], picked)
    return picked


def exchange_shared(shared_cache, group_ids, req_index, req_count):
    received = [pick_group(shared_cache, group_ids, req_index)]
    pow2 = req_count & (req_count - 1) == 0
    for k in range(1, req_count):
        if pow2:
            pairs = [(r, r ^ k) for r in range(req_count)]
            dst = req_index ^ k
        else:
            pairs = [(r, (r + k) % req_count) for r in range(req_count)]
            dst = (req_index + k) % req_count
        sent = pick_group(shared_cache, group_ids, dst)
        received.append(lax.ppermute(sent, "req", pairs))
    return received


def split16(x):
    high = x.astype(jnp.bfloat16)
    low = (x - high.astype(jnp.float32)).astype(jnp.bfloat16)
    return high, low


def join16(high, low):
    return high.astype(jnp.float32) + low.astype(jnp.float32)


def shards(
    draft_query,
    draft_kv,
    own_cache,
    shared_cache,
    out_weight,
    lengths,
    group_ids,
    parents,
    accepted,
):
    kv_heads = own_cache.shape[3] // HD
    draft_len = draft_query.shape[1]
    rows = QPK * draft_len
    seq_count = lax.axis_size("seq")
    seq_index = lax.axis_index("seq")
    req_index = lax.axis_index("req")
    req_count = lax.axis_size("req")
    cache_len = own_cache.shape[2]

    blocks = exchange_shared(shared_cache, group_ids, req_index, req_count)

    queries = (
        draft_query[0]
        .reshape(draft_len, kv_heads, QPK, HD)
        .transpose(1, 2, 0, 3)
        .reshape(kv_heads, rows, HD)
    )
    n_valid = jnp.clip(lengths[0] - seq_index * cache_len, 0, cache_len).astype(jnp.int32)
    state = own_attend(queries, own_cache[0], n_valid.reshape(1))

    reach = tree_reach(parents[0])
    reach_rows = jnp.tile(reach.astype(jnp.float32), (QPK, 1))
    flag = (seq_index == 0).astype(jnp.int32).reshape(1)
    state = shared_attend(queries, state, blocks[:1], (draft_kv[0], reach_rows, flag))
    for blk in blocks[1:]:
        state = shared_attend(queries, state, [blk])
    m, l, acc = state

    heads_dev = kv_heads * QPK
    share = heads_dev // seq_count
    part_out = (acc / l).astype(jnp.bfloat16).reshape(heads_dev, draft_len, HD)
    m_hi, m_lo = split16(m[..., 0].reshape(heads_dev, draft_len))
    l_hi, l_lo = split16(l[..., 0].reshape(heads_dev, draft_len))
    stats = jnp.stack(
        [jnp.concatenate([m_hi, m_lo], 1), jnp.concatenate([l_hi, l_lo], 1)], 1
    )
    packed = jnp.concatenate([part_out, stats], 1)
    packed = lax.all_to_all(packed, "seq", 0, 0, tiled=True)
    packed = packed.reshape(seq_count, share, draft_len + 2, 2 * draft_len)
    part_max = join16(packed[:, :, draft_len, :draft_len], packed[:, :, draft_len, draft_len:])
    part_total = join16(
        packed[:, :, draft_len + 1, :draft_len], packed[:, :, draft_len + 1, draft_len:]
    )
    part_sum = packed[:, :, :draft_len, :].astype(jnp.float32)
    final_max = jnp.max(part_max, axis=0)
    factor = jnp.exp2((part_max - final_max[None]) * EXP2_SCALE) * part_total
    final_total = jnp.sum(factor, axis=0)
    final_sum = jnp.sum(part_sum * factor[..., None], axis=0)
    attended = (final_sum / final_total[..., None]).astype(jnp.bfloat16)
    attended = jnp.transpose(attended, (1, 0, 2)).reshape(draft_len, share * HD)
    out_group = ("tensor", "seq")
    owners = lax.axis_size("tensor") * seq_count
    columns = out_weight.shape[1] // owners
    product = jnp.einsum(
        "ik,kcj->cij",
        attended,
        out_weight.reshape(out_weight.shape[0], owners, columns),
        preferred_element_type=jnp.float32,
    ).astype(jnp.bfloat16)
    pieces = lax.all_to_all(product, out_group, 0, 0, tiled=True)
    verified = jnp.sum(pieces.astype(jnp.float32), axis=0).astype(jnp.bfloat16)[None]
    accepted_kv = jnp.take(draft_kv[0], accepted[0], axis=1)[None]
    return (verified, accepted_kv)


def solution(mesh):
    placed = (
        P("req", None, "tensor"),
        P("req", None, None, "tensor"),
        P("req", None, "seq", "tensor"),
        P(None, None, ("req", "seq"), "tensor"),
        P(("tensor", "seq"), None),
        P("req"),
        P(),
        P("req", None),
        P("req", None),
    )
    return jax.shard_map(
        shards,
        mesh=mesh,
        in_specs=placed,
        out_specs=(P("req", None, ("tensor", "seq")), P("req", None, None, "tensor")),
        check_vma=False,
    )
```

```python
import functools

import jax
import jax.numpy as jnp
from jax import lax
from jax.experimental import pallas as pl
from jax.experimental.pallas import tpu as pltpu
from jax.sharding import PartitionSpec as P

HD = 128
QPK = 8
NEG_FILL = -1e30
SCALE = HD ** (-0.5)
EXP2_SCALE = SCALE * 1.4426950408889634
OWN_BLOCK = 512


def step(m_prev, l_prev, acc_prev, q, k, v, ones, ok):
    scores = lax.dot_general(
        q, k, (((1,), (1,)), ((), ())), preferred_element_type=jnp.float32
    )
    if ok is not None:
        scores = jnp.where(ok, scores, NEG_FILL)
    m_new = jnp.maximum(m_prev, jnp.max(scores, axis=1, keepdims=True))
    alpha = jnp.exp2((m_prev - m_new) * EXP2_SCALE)
    weights = jnp.exp2((scores - m_new) * EXP2_SCALE)
    if ok is not None:
        weights = jnp.where(ok, weights, 0.0)
    weights = weights.astype(jnp.bfloat16)
    l_new = alpha * l_prev + jnp.dot(weights, ones, preferred_element_type=jnp.float32)
    acc_new = alpha * acc_prev + jnp.dot(weights, v, preferred_element_type=jnp.float32)
    return m_new, l_new, acc_new


def own_kernel(kv_heads, block, nv_ref, q_ref, kv_ref, ones_ref, m_out, l_out, acc_out, m_s, l_s, acc_s):
    j = pl.program_id(0)
    n_valid = nv_ref[0]

    @pl.when(j == 0)
    def _():
        m_s[...] = jnp.full(m_s.shape, NEG_FILL, jnp.float32)
        l_s[...] = jnp.zeros(l_s.shape, jnp.float32)
        acc_s[...] = jnp.zeros(acc_s.shape, jnp.float32)

    start = j * block

    def body(masked):
        ok = None
        if masked:
            cols = start + lax.broadcasted_iota(jnp.int32, (1, block), 1)
            ok = cols < n_valid
        for h in range(kv_heads):
            cols_h = slice(h * HD, (h + 1) * HD)
            m, l, acc = step(
                m_s[h], l_s[h], acc_s[h], q_ref[h], kv_ref[0, :, cols_h], kv_ref[1, :, cols_h],
                ones_ref[...], ok,
            )
            m_s[h] = m
            l_s[h] = l
            acc_s[h] = acc

    full = start + block <= n_valid
    part = jnp.logical_and(start < n_valid, jnp.logical_not(full))
    pl.when(full)(lambda: body(False))
    pl.when(part)(lambda: body(True))

    @pl.when(j == pl.num_programs(0) - 1)
    def _():
        m_out[...] = m_s[...]
        l_out[...] = l_s[...]
        acc_out[...] = acc_s[...]


def own_attend(q, kv, n_valid):
    kv_heads, rows, _ = q.shape
    cache_len = kv.shape[1]
    block = min(OWN_BLOCK, cache_len)
    n_blocks = cache_len // block

    def kv_map(j, nv):
        last = jnp.maximum((nv[0] + block - 1) // block - 1, 0)
        return (0, jnp.minimum(j, last), 0)

    state_shapes = (
        jax.ShapeDtypeStruct((kv_heads, rows, 1), jnp.float32),
        jax.ShapeDtypeStruct((kv_heads, rows, HD), jnp.float32),
        jax.ShapeDtypeStruct((kv_heads, rows, HD), jnp.float32),
    )
    ones = jnp.ones((block, HD), jnp.bfloat16)
    full3 = lambda j, nv: (0, 0, 0)
    return pl.pallas_call(
        functools.partial(own_kernel, kv_heads, block),
        out_shape=state_shapes,
        grid_spec=pltpu.PrefetchScalarGridSpec(
            num_scalar_prefetch=1,
            grid=(n_blocks,),
            in_specs=[
                pl.BlockSpec(q.shape, full3),
                pl.BlockSpec((2, block, kv.shape[2]), kv_map),
                pl.BlockSpec(ones.shape, lambda j, nv: (0, 0)),
            ],
            out_specs=[pl.BlockSpec(s.shape, full3) for s in state_shapes],
            scratch_shapes=[pltpu.VMEM(s.shape, jnp.float32) for s in state_shapes],
        ),
        compiler_params=pltpu.CompilerParams(dimension_semantics=("arbitrary",)),
        cost_estimate=pl.CostEstimate(
            flops=6 * kv_heads * rows * cache_len * HD,
            transcendentals=kv_heads * rows * cache_len,
            bytes_accessed=kv.size * 2 + q.size * 2,
        ),
    )(n_valid, q, kv, ones)


def shared_kernel(kv_heads, n_blocks, with_tree, flag_ref, q_ref, m_ref, l_ref, acc_ref, *rest):
    blocks = rest[:n_blocks]
    ones_ref = rest[n_blocks]
    rest = rest[n_blocks + 1:]
    if with_tree:
        dkv_ref, reach_ref, tree_ones_ref = rest[:3]
        rest = rest[3:]
    m_out, l_out, acc_out = rest[:3]
    for h in range(kv_heads):
        cols_h = slice(h * HD, (h + 1) * HD)
        q = q_ref[h]
        m, l, acc = m_ref[h], l_ref[h], acc_ref[h]
        for blk in blocks:
            m, l, acc = step(
                m, l, acc, q, blk[0, :, cols_h], blk[1, :, cols_h], ones_ref[...], None
            )
        m_out[h] = m
        l_out[h] = l
        acc_out[h] = acc

    if with_tree:
        @pl.when(flag_ref[0] == 1)
        def _():
            ok = reach_ref[...] > 0.5
            for h in range(kv_heads):
                cols_h = slice(h * HD, (h + 1) * HD)
                m, l, acc = step(
                    m_out[h], l_out[h], acc_out[h], q_ref[h],
                    dkv_ref[0, :, cols_h], dkv_ref[1, :, cols_h], tree_ones_ref[...], ok,
                )
                m_out[h] = m
                l_out[h] = l
                acc_out[h] = acc


def shared_attend(q, state, blocks, tree=None):
    kv_heads, rows, _ = q.shape
    n_blocks = len(blocks)
    whole = lambda a: pl.BlockSpec(a.shape, lambda i, f: (0,) * a.ndim)
    ones = jnp.ones((blocks[0].shape[1], HD), jnp.bfloat16)
    operands = (q,) + tuple(state) + tuple(blocks) + (ones,)
    if tree is not None:
        draft_kv, reach_rows, flag = tree
        operands += (draft_kv, reach_rows, jnp.ones((draft_kv.shape[1], HD), jnp.bfloat16))
    else:
        flag = jnp.zeros((1,), jnp.int32)
    keys = sum(b.shape[1] for b in blocks)
    return pl.pallas_call(
        functools.partial(shared_kernel, kv_heads, n_blocks, tree is not None),
        out_shape=tuple(jax.ShapeDtypeStruct(s.shape, s.dtype) for s in state),
        grid_spec=pltpu.PrefetchScalarGridSpec(
            num_scalar_prefetch=1,
            grid=(1,),
            in_specs=[whole(a) for a in operands],
            out_specs=[whole(s) for s in state],
        ),
        compiler_params=pltpu.CompilerParams(vmem_limit_bytes=48 * 1024 * 1024),
        cost_estimate=pl.CostEstimate(
            flops=6 * kv_heads * rows * keys * HD,
            transcendentals=kv_heads * rows * keys,
            bytes_accessed=sum(b.size * 2 for b in blocks) + q.size * 2,
        ),
    )(flag, *operands)


def tree_reach(parent_row):
    node_count = parent_row.shape[0]
    nodes = jnp.arange(node_count, dtype=jnp.int32)
    reach = jnp.eye(node_count, dtype=jnp.float32) + (parent_row[:, None] == nodes[None, :]).astype(
        jnp.float32
    )
    for level_step in range(max(node_count - 1, 1).bit_length()):
        reach = jnp.minimum(jnp.dot(reach, reach, precision=lax.Precision.HIGHEST), 1.0)
    return reach > 0.5


def pick_group(shared_cache, group_ids, request):
    onehot = jnp.arange(group_ids.shape[0], dtype=jnp.int32) == request
    group = jnp.sum(jnp.where(onehot, group_ids, 0))
    picked = shared_cache[:, 0]
    for g in range(1, shared_cache.shape[1]):
        picked = jnp.where(group == g, shared_cache[:, g], picked)
    return picked


def exchange_shared(shared_cache, group_ids, req_index, req_count):
    received = [pick_group(shared_cache, group_ids, req_index)]
    pow2 = req_count & (req_count - 1) == 0
    for k in range(1, req_count):
        if pow2:
            pairs = [(r, r ^ k) for r in range(req_count)]
            dst = req_index ^ k
        else:
            pairs = [(r, (r + k) % req_count) for r in range(req_count)]
            dst = (req_index + k) % req_count
        sent = pick_group(shared_cache, group_ids, dst)
        received.append(lax.ppermute(sent, "req", pairs))
    return received


def split16(x):
    high = lax.reduce_precision(x, exponent_bits=8, mantissa_bits=7)
    low = (x - high).astype(jnp.bfloat16)
    return high.astype(jnp.bfloat16), low


def join16(high, low):
    return high.astype(jnp.float32) + low.astype(jnp.float32)


def shards(
    draft_query,
    draft_kv,
    own_cache,
    shared_cache,
    out_weight,
    lengths,
    group_ids,
    parents,
    accepted,
):
    kv_heads = own_cache.shape[3] // HD
    draft_len = draft_query.shape[1]
    rows = QPK * draft_len
    seq_count = lax.axis_size("seq")
    seq_index = lax.axis_index("seq")
    req_index = lax.axis_index("req")
    req_count = lax.axis_size("req")
    cache_len = own_cache.shape[2]

    blocks = exchange_shared(shared_cache, group_ids, req_index, req_count)

    queries = (
        draft_query[0]
        .reshape(draft_len, kv_heads, QPK, HD)
        .transpose(1, 2, 0, 3)
        .reshape(kv_heads, rows, HD)
    )
    n_valid = jnp.clip(lengths[0] - seq_index * cache_len, 0, cache_len).astype(jnp.int32)
    state = own_attend(queries, own_cache[0], n_valid.reshape(1))

    reach = tree_reach(parents[0])
    reach_rows = jnp.tile(reach.astype(jnp.float32), (QPK, 1))
    flag = (seq_index == 0).astype(jnp.int32).reshape(1)
    state = shared_attend(queries, state, blocks[:1], (draft_kv[0], reach_rows, flag))
    for blk in blocks[1:]:
        state = shared_attend(queries, state, [blk])
    m, l, acc = state

    heads_dev = kv_heads * QPK
    share = heads_dev // seq_count
    part_out = (acc / l).astype(jnp.bfloat16).reshape(heads_dev, draft_len, HD)
    m_hi, m_lo = split16(m[..., 0].reshape(heads_dev, draft_len))
    l_hi, l_lo = split16(l[..., 0].reshape(heads_dev, draft_len))
    stats = jnp.stack(
        [jnp.concatenate([m_hi, m_lo], 1), jnp.concatenate([l_hi, l_lo], 1)], 1
    )
    packed = jnp.concatenate([part_out, stats], 1)
    packed = lax.all_to_all(packed, "seq", 0, 0, tiled=True)
    packed = packed.reshape(seq_count, share, draft_len + 2, 2 * draft_len)
    part_max = join16(packed[:, :, draft_len, :draft_len], packed[:, :, draft_len, draft_len:])
    part_total = join16(
        packed[:, :, draft_len + 1, :draft_len], packed[:, :, draft_len + 1, draft_len:]
    )
    part_sum = packed[:, :, :draft_len, :].astype(jnp.float32)
    final_max = jnp.max(part_max, axis=0)
    factor = jnp.exp2((part_max - final_max[None]) * EXP2_SCALE) * part_total
    final_total = jnp.sum(factor, axis=0)
    final_sum = jnp.sum(part_sum * factor[..., None], axis=0)
    attended = (final_sum / final_total[..., None]).astype(jnp.bfloat16)
    attended = jnp.transpose(attended, (1, 0, 2)).reshape(draft_len, share * HD)
    out_group = ("tensor", "seq")
    owners = lax.axis_size("tensor") * seq_count
    columns = out_weight.shape[1] // owners
    product = jnp.einsum(
        "ik,kcj->cij",
        attended,
        out_weight.reshape(out_weight.shape[0], owners, columns),
        preferred_element_type=jnp.float32,
    ).astype(jnp.bfloat16)
    pieces = lax.all_to_all(product, out_group, 0, 0, tiled=True)
    verified = jnp.sum(pieces.astype(jnp.float32), axis=0).astype(jnp.bfloat16)[None]
    accepted_kv = jnp.take(draft_kv[0], accepted[0], axis=1)[None]
    return (verified, accepted_kv)


def solution(mesh):
    placed = (
        P("req", None, "tensor"),
        P("req", None, None, "tensor"),
        P("req", None, "seq", "tensor"),
        P(None, None, ("req", "seq"), "tensor"),
        P(("tensor", "seq"), None),
        P("req"),
        P(),
        P("req", None),
        P("req", None),
    )
    return jax.shard_map(
        shards,
        mesh=mesh,
        in_specs=placed,
        out_specs=(P("req", None, ("tensor", "seq")), P("req", None, None, "tensor")),
        check_vma=False,
    )
```

```python
import functools

import jax
import jax.numpy as jnp
from jax import lax
from jax.experimental import pallas as pl
from jax.experimental.pallas import tpu as pltpu
from jax.sharding import PartitionSpec as P


HD = 128
QPK = 8
NEG_FILL = -1e30
SCALE = HD ** (-0.5)
EXP2_SCALE = SCALE * 1.4426950408889634
OWN_BLOCK = 1024


def step(m_prev, l_prev, acc_prev, q, k, v, ones, ok):
    scores = lax.dot_general(
        q, k, (((1,), (1,)), ((), ())), preferred_element_type=jnp.float32
    )
    if ok is not None:
        scores = jnp.where(ok, scores, NEG_FILL)
    m_new = jnp.maximum(m_prev, jnp.max(scores, axis=1, keepdims=True))
    alpha = jnp.exp2((m_prev - m_new) * EXP2_SCALE)
    weights = jnp.exp2((scores - m_new) * EXP2_SCALE)
    if ok is not None:
        weights = jnp.where(ok, weights, 0.0)
    weights = weights.astype(jnp.bfloat16)
    l_new = alpha * l_prev + jnp.dot(weights, ones, preferred_element_type=jnp.float32)
    acc_new = alpha * acc_prev + jnp.dot(weights, v, preferred_element_type=jnp.float32)
    return m_new, l_new, acc_new


def own_kernel(kv_heads, block, nv_ref, q_ref, kv_ref, ones_ref, m_out, l_out, acc_out, m_s, l_s, acc_s):
    j = pl.program_id(0)
    n_valid = nv_ref[0]

    @pl.when(j == 0)
    def _():
        m_s[...] = jnp.full(m_s.shape, NEG_FILL, jnp.float32)
        l_s[...] = jnp.zeros(l_s.shape, jnp.float32)
        acc_s[...] = jnp.zeros(acc_s.shape, jnp.float32)

    start = j * block

    def body(masked):
        ok = None
        if masked:
            cols = start + lax.broadcasted_iota(jnp.int32, (1, block), 1)
            ok = cols < n_valid
        for h in range(kv_heads):
            cols_h = slice(h * HD, (h + 1) * HD)
            m, l, acc = step(
                m_s[h], l_s[h], acc_s[h], q_ref[h], kv_ref[0, :, cols_h], kv_ref[1, :, cols_h],
                ones_ref[...], ok,
            )
            m_s[h] = m
            l_s[h] = l
            acc_s[h] = acc

    full = start + block <= n_valid
    part = jnp.logical_and(start < n_valid, jnp.logical_not(full))
    pl.when(full)(lambda: body(False))
    pl.when(part)(lambda: body(True))

    @pl.when(j == pl.num_programs(0) - 1)
    def _():
        m_out[...] = m_s[...]
        l_out[...] = l_s[...]
        acc_out[...] = acc_s[...]


def own_attend(q, kv, n_valid):
    kv_heads, rows, _ = q.shape
    cache_len = kv.shape[1]
    block = min(OWN_BLOCK, cache_len)
    n_blocks = cache_len // block

    def kv_map(j, nv):
        last = jnp.maximum((nv[0] + block - 1) // block - 1, 0)
        return (0, jnp.minimum(j, last), 0)

    state_shapes = (
        jax.ShapeDtypeStruct((kv_heads, rows, 1), jnp.float32),
        jax.ShapeDtypeStruct((kv_heads, rows, HD), jnp.float32),
        jax.ShapeDtypeStruct((kv_heads, rows, HD), jnp.float32),
    )
    ones = jnp.ones((block, HD), jnp.bfloat16)
    full3 = lambda j, nv: (0, 0, 0)
    return pl.pallas_call(
        functools.partial(own_kernel, kv_heads, block),
        out_shape=state_shapes,
        grid_spec=pltpu.PrefetchScalarGridSpec(
            num_scalar_prefetch=1,
            grid=(n_blocks,),
            in_specs=[
                pl.BlockSpec(q.shape, full3),
                pl.BlockSpec((2, block, kv.shape[2]), kv_map),
                pl.BlockSpec(ones.shape, lambda j, nv: (0, 0)),
            ],
            out_specs=[pl.BlockSpec(s.shape, full3) for s in state_shapes],
            scratch_shapes=[pltpu.VMEM(s.shape, jnp.float32) for s in state_shapes],
        ),
        compiler_params=pltpu.CompilerParams(dimension_semantics=("arbitrary",)),
        cost_estimate=pl.CostEstimate(
            flops=6 * kv_heads * rows * cache_len * HD,
            transcendentals=kv_heads * rows * cache_len,
            bytes_accessed=kv.size * 2 + q.size * 2,
        ),
    )(n_valid, q, kv, ones)


def shared_kernel(kv_heads, n_blocks, with_tree, flag_ref, q_ref, m_ref, l_ref, acc_ref, *rest):
    blocks = rest[:n_blocks]
    ones_ref = rest[n_blocks]
    rest = rest[n_blocks + 1:]
    if with_tree:
        dkv_ref, reach_ref, tree_ones_ref = rest[:3]
        rest = rest[3:]
    m_out, l_out, acc_out = rest[:3]
    for h in range(kv_heads):
        cols_h = slice(h * HD, (h + 1) * HD)
        q = q_ref[h]
        m, l, acc = m_ref[h], l_ref[h], acc_ref[h]
        for blk in blocks:
            m, l, acc = step(
                m, l, acc, q, blk[0, :, cols_h], blk[1, :, cols_h], ones_ref[...], None
            )
        m_out[h] = m
        l_out[h] = l
        acc_out[h] = acc

    if with_tree:
        @pl.when(flag_ref[0] == 1)
        def _():
            ok = reach_ref[...] > 0.5
            for h in range(kv_heads):
                cols_h = slice(h * HD, (h + 1) * HD)
                m, l, acc = step(
                    m_out[h], l_out[h], acc_out[h], q_ref[h],
                    dkv_ref[0, :, cols_h], dkv_ref[1, :, cols_h], tree_ones_ref[...], ok,
                )
                m_out[h] = m
                l_out[h] = l
                acc_out[h] = acc


def shared_attend(q, state, blocks, tree=None):
    kv_heads, rows, _ = q.shape
    n_blocks = len(blocks)
    whole = lambda a: pl.BlockSpec(a.shape, lambda i, f: (0,) * a.ndim)
    ones = jnp.ones((blocks[0].shape[1], HD), jnp.bfloat16)
    operands = (q,) + tuple(state) + tuple(blocks) + (ones,)
    if tree is not None:
        draft_kv, reach_rows, flag = tree
        operands += (draft_kv, reach_rows, jnp.ones((draft_kv.shape[1], HD), jnp.bfloat16))
    else:
        flag = jnp.zeros((1,), jnp.int32)
    keys = sum(b.shape[1] for b in blocks)
    return pl.pallas_call(
        functools.partial(shared_kernel, kv_heads, n_blocks, tree is not None),
        out_shape=tuple(jax.ShapeDtypeStruct(s.shape, s.dtype) for s in state),
        grid_spec=pltpu.PrefetchScalarGridSpec(
            num_scalar_prefetch=1,
            grid=(1,),
            in_specs=[whole(a) for a in operands],
            out_specs=[whole(s) for s in state],
        ),
        compiler_params=pltpu.CompilerParams(vmem_limit_bytes=48 * 1024 * 1024),
        cost_estimate=pl.CostEstimate(
            flops=6 * kv_heads * rows * keys * HD,
            transcendentals=kv_heads * rows * keys,
            bytes_accessed=sum(b.size * 2 for b in blocks) + q.size * 2,
        ),
    )(flag, *operands)


def tree_reach(parent_row):
    node_count = parent_row.shape[0]
    nodes = jnp.arange(node_count, dtype=jnp.int32)
    reach = jnp.eye(node_count, dtype=jnp.float32) + (parent_row[:, None] == nodes[None, :]).astype(
        jnp.float32
    )
    for _ in range(max(node_count - 1, 1).bit_length()):
        reach = jnp.minimum(jnp.dot(reach, reach, precision=lax.Precision.HIGHEST), 1.0)
    return reach > 0.5


def pick_group(shared_cache, group_ids, request):
    onehot = jnp.arange(group_ids.shape[0], dtype=jnp.int32) == request
    group = jnp.sum(jnp.where(onehot, group_ids, 0))
    picked = shared_cache[:, 0]
    for g in range(1, shared_cache.shape[1]):
        picked = jnp.where(group == g, shared_cache[:, g], picked)
    return picked


def partner(index, k, count):
    if count & (count - 1) == 0:
        return index ^ k
    return (index + k) % count


def exchange_shared(shared_cache, group_ids, req_index, req_count, distances):
    received = [pick_group(shared_cache, group_ids, req_index)]
    for k in distances:
        pairs = [(r, partner(r, k, req_count)) for r in range(req_count)]
        sent = pick_group(shared_cache, group_ids, partner(req_index, k, req_count))
        received.append(lax.ppermute(sent, "req", pairs))
    return received


def exchange_to_owner(shared_cache, group_ids, req_index, seq_index, req_count, seq_count, k):
    picked = pick_group(shared_cache, group_ids, partner(req_index, k, req_count))
    received = []
    for d in range(seq_count):
        head = partner(seq_index, d, seq_count)
        piece = lax.dynamic_slice_in_dim(picked, head * HD, HD, 2)
        pairs = [
            (r * seq_count + q, partner(r, k, req_count) * seq_count + partner(q, d, seq_count))
            for r in range(req_count)
            for q in range(seq_count)
        ]
        received.append(lax.ppermute(piece, ("req", "seq"), pairs))
    return received


def split16(x):
    high = lax.reduce_precision(x, exponent_bits=8, mantissa_bits=7)
    low = (x - high).astype(jnp.bfloat16)
    return high.astype(jnp.bfloat16), low


def join16(high, low):
    return high.astype(jnp.float32) + low.astype(jnp.float32)


def layer(
    draft_query,
    draft_kv,
    own_cache,
    shared_cache,
    out_weight,
    lengths,
    group_ids,
    parents,
    accepted,
):
    kv_heads = own_cache.shape[3] // HD
    draft_len = draft_query.shape[1]
    rows = QPK * draft_len
    seq_count = lax.axis_size("seq")
    seq_index = lax.axis_index("seq")
    req_index = lax.axis_index("req")
    req_count = lax.axis_size("req")
    cache_len = own_cache.shape[2]

    distances = list(range(1, req_count))
    owner_mode = kv_heads == seq_count and len(distances) > 0
    if owner_mode:
        owner_blocks = exchange_to_owner(
            shared_cache, group_ids, req_index, seq_index, req_count, seq_count, distances[-1]
        )
        distances = distances[:-1]
    blocks = exchange_shared(shared_cache, group_ids, req_index, req_count, distances)

    queries = (
        draft_query[0]
        .reshape(draft_len, kv_heads, QPK, HD)
        .transpose(1, 2, 0, 3)
        .reshape(kv_heads, rows, HD)
    )
    n_valid = jnp.clip(lengths[0] - seq_index * cache_len, 0, cache_len).astype(jnp.int32)
    state = own_attend(queries, own_cache[0], n_valid.reshape(1))

    reach = tree_reach(parents[0])
    reach_rows = jnp.tile(reach.astype(jnp.float32), (QPK, 1))
    flag = (seq_index == 0).astype(jnp.int32).reshape(1)
    state = shared_attend(queries, state, blocks[:1], (draft_kv[0], reach_rows, flag))
    for blk in blocks[1:]:
        state = shared_attend(queries, state, [blk])
    m, l, acc = state

    heads_dev = kv_heads * QPK
    share = heads_dev // seq_count
    part_out = (acc / l).astype(jnp.bfloat16).reshape(heads_dev, draft_len, HD)
    m_hi, m_lo = split16(m[..., 0].reshape(heads_dev, draft_len))
    l_hi, l_lo = split16(l[..., 0].reshape(heads_dev, draft_len))
    stats = jnp.stack(
        [jnp.concatenate([m_hi, m_lo], 1), jnp.concatenate([l_hi, l_lo], 1)], 1
    )
    packed = jnp.concatenate([part_out, stats], 1)
    packed = lax.all_to_all(packed, "seq", 0, 0, tiled=True)
    packed = packed.reshape(seq_count, share, draft_len + 2, 2 * draft_len)
    part_max = join16(packed[:, :, draft_len, :draft_len], packed[:, :, draft_len, draft_len:])
    part_total = join16(
        packed[:, :, draft_len + 1, :draft_len], packed[:, :, draft_len + 1, draft_len:]
    )
    part_sum = packed[:, :, :draft_len, :].astype(jnp.float32)
    final_max = jnp.max(part_max, axis=0)
    factor = jnp.exp2((part_max - final_max[None]) * EXP2_SCALE) * part_total
    final_total = jnp.sum(factor, axis=0)
    final_sum = jnp.sum(part_sum * factor[..., None], axis=0)
    if owner_mode:
        rows_owned = share * draft_len
        owned_query = lax.dynamic_index_in_dim(queries, seq_index, 0, keepdims=True)
        owned_state = (
            final_max.reshape(1, rows_owned, 1),
            jnp.broadcast_to(final_total.reshape(1, rows_owned, 1), (1, rows_owned, HD)),
            final_sum.reshape(1, rows_owned, HD),
        )
        _, owned_total, owned_sum = shared_attend(owned_query, owned_state, owner_blocks)
        attended = (owned_sum / owned_total).reshape(share, draft_len, HD).astype(jnp.bfloat16)
    else:
        attended = (final_sum / final_total[..., None]).astype(jnp.bfloat16)
    attended = jnp.transpose(attended, (1, 0, 2)).reshape(draft_len, share * HD)
    out_group = ("tensor", "seq")
    owners = lax.axis_size("tensor") * seq_count
    columns = out_weight.shape[1] // owners
    product = jnp.einsum(
        "ik,kcj->cij",
        attended,
        out_weight.reshape(out_weight.shape[0], owners, columns),
        preferred_element_type=jnp.float32,
    ).astype(jnp.bfloat16)
    pieces = lax.all_to_all(product, out_group, 0, 0, tiled=True)
    verified = jnp.sum(pieces.astype(jnp.float32), axis=0).astype(jnp.bfloat16)[None]
    accepted_kv = jnp.take(draft_kv[0], accepted[0], axis=1)[None]
    return (verified, accepted_kv)


def solution(mesh):
    placed = (
        P("req", None, "tensor"),
        P("req", None, None, "tensor"),
        P("req", None, "seq", "tensor"),
        P(None, None, ("req", "seq"), "tensor"),
        P(("tensor", "seq"), None),
        P("req"),
        P(),
        P("req", None),
        P("req", None),
    )
    return jax.shard_map(
        layer,
        mesh=mesh,
        in_specs=placed,
        out_specs=(P("req", None, ("tensor", "seq")), P("req", None, None, "tensor")),
        check_vma=False,
    )
```

```python
import functools

import jax
import jax.numpy as jnp
from jax import lax
from jax.experimental import pallas as pl
from jax.experimental.pallas import tpu as pltpu
from jax.sharding import PartitionSpec as P


HD = 128
QPK = 8
NEG_FILL = -1e30
SCALE = HD ** (-0.5)
EXP2_SCALE = SCALE * 1.4426950408889634
OWN_BLOCK = 2048


def step(m_prev, l_prev, acc_prev, q, k, v, ones, ok):
    scores = lax.dot_general(
        q, k, (((1,), (1,)), ((), ())), preferred_element_type=jnp.float32
    )
    if ok is not None:
        scores = jnp.where(ok, scores, NEG_FILL)
    m_new = jnp.maximum(m_prev, jnp.max(scores, axis=1, keepdims=True))
    alpha = jnp.exp2((m_prev - m_new) * EXP2_SCALE)
    weights = jnp.exp2((scores - m_new) * EXP2_SCALE)
    if ok is not None:
        weights = jnp.where(ok, weights, 0.0)
    weights = weights.astype(jnp.bfloat16)
    l_new = alpha * l_prev + jnp.dot(weights, ones, preferred_element_type=jnp.float32)
    acc_new = alpha * acc_prev + jnp.dot(weights, v, preferred_element_type=jnp.float32)
    return m_new, l_new, acc_new


def own_kernel(kv_heads, block, nv_ref, q_ref, kv_ref, ones_ref, m_out, l_out, acc_out, m_s, l_s, acc_s):
    j = pl.program_id(0)
    n_valid = nv_ref[0]

    @pl.when(j == 0)
    def _():
        m_s[...] = jnp.full(m_s.shape, NEG_FILL, jnp.float32)
        l_s[...] = jnp.zeros(l_s.shape, jnp.float32)
        acc_s[...] = jnp.zeros(acc_s.shape, jnp.float32)

    start = j * block

    def body(masked):
        ok = None
        if masked:
            cols = start + lax.broadcasted_iota(jnp.int32, (1, block), 1)
            ok = cols < n_valid

        def head(h, carry):
            cols_h = pl.ds(pl.multiple_of(h * HD, HD), HD)
            m, l, acc = step(
                m_s[h], l_s[h], acc_s[h], q_ref[h], kv_ref[0, :, cols_h], kv_ref[1, :, cols_h],
                ones_ref[...], ok,
            )
            m_s[h] = m
            l_s[h] = l
            acc_s[h] = acc
            return carry

        lax.fori_loop(0, kv_heads, head, 0)

    full = start + block <= n_valid
    part = jnp.logical_and(start < n_valid, jnp.logical_not(full))
    pl.when(full)(lambda: body(False))
    pl.when(part)(lambda: body(True))

    @pl.when(j == pl.num_programs(0) - 1)
    def _():
        m_out[...] = m_s[...]
        l_out[...] = l_s[...]
        acc_out[...] = acc_s[...]


def own_attend(q, kv, n_valid):
    kv_heads, rows, _ = q.shape
    cache_len = kv.shape[1]
    block = min(OWN_BLOCK, cache_len)
    n_blocks = cache_len // block

    def kv_map(j, nv):
        last = jnp.maximum((nv[0] + block - 1) // block - 1, 0)
        return (0, jnp.minimum(j, last), 0)

    state_shapes = (
        jax.ShapeDtypeStruct((kv_heads, rows, 1), jnp.float32),
        jax.ShapeDtypeStruct((kv_heads, rows, HD), jnp.float32),
        jax.ShapeDtypeStruct((kv_heads, rows, HD), jnp.float32),
    )
    ones = jnp.ones((block, HD), jnp.bfloat16)
    full3 = lambda j, nv: (0, 0, 0)
    return pl.pallas_call(
        functools.partial(own_kernel, kv_heads, block),
        out_shape=state_shapes,
        grid_spec=pltpu.PrefetchScalarGridSpec(
            num_scalar_prefetch=1,
            grid=(n_blocks,),
            in_specs=[
                pl.BlockSpec(q.shape, full3),
                pl.BlockSpec((2, block, kv.shape[2]), kv_map),
                pl.BlockSpec(ones.shape, lambda j, nv: (0, 0)),
            ],
            out_specs=[pl.BlockSpec(s.shape, full3) for s in state_shapes],
            scratch_shapes=[pltpu.VMEM(s.shape, jnp.float32) for s in state_shapes],
        ),
        compiler_params=pltpu.CompilerParams(dimension_semantics=("arbitrary",)),
        cost_estimate=pl.CostEstimate(
            flops=6 * kv_heads * rows * cache_len * HD,
            transcendentals=kv_heads * rows * cache_len,
            bytes_accessed=kv.size * 2 + q.size * 2,
        ),
    )(n_valid, q, kv, ones)


def shared_kernel(kv_heads, n_blocks, with_tree, flag_ref, q_ref, m_ref, l_ref, acc_ref, *rest):
    blocks = rest[:n_blocks]
    ones_ref = rest[n_blocks]
    rest = rest[n_blocks + 1:]
    if with_tree:
        dkv_ref, reach_ref, tree_ones_ref = rest[:3]
        rest = rest[3:]
    m_out, l_out, acc_out = rest[:3]

    def head(h, carry):
        cols_h = pl.ds(pl.multiple_of(h * HD, HD), HD)
        q = q_ref[h]
        m, l, acc = m_ref[h], l_ref[h], acc_ref[h]
        for blk in blocks:
            m, l, acc = step(
                m, l, acc, q, blk[0, :, cols_h], blk[1, :, cols_h], ones_ref[...], None
            )
        m_out[h] = m
        l_out[h] = l
        acc_out[h] = acc
        return carry

    lax.fori_loop(0, kv_heads, head, 0)

    if with_tree:
        @pl.when(flag_ref[0] == 1)
        def _():
            ok = reach_ref[...] > 0.5
            for h in range(kv_heads):
                cols_h = slice(h * HD, (h + 1) * HD)
                m, l, acc = step(
                    m_out[h], l_out[h], acc_out[h], q_ref[h],
                    dkv_ref[0, :, cols_h], dkv_ref[1, :, cols_h], tree_ones_ref[...], ok,
                )
                m_out[h] = m
                l_out[h] = l
                acc_out[h] = acc


def shared_attend(q, state, blocks, tree=None):
    kv_heads, rows, _ = q.shape
    n_blocks = len(blocks)
    whole = lambda a: pl.BlockSpec(a.shape, lambda i, f: (0,) * a.ndim)
    ones = jnp.ones((blocks[0].shape[1], HD), jnp.bfloat16)
    operands = (q,) + tuple(state) + tuple(blocks) + (ones,)
    if tree is not None:
        draft_kv, reach_rows, flag = tree
        operands += (draft_kv, reach_rows, jnp.ones((draft_kv.shape[1], HD), jnp.bfloat16))
    else:
        flag = jnp.zeros((1,), jnp.int32)
    keys = sum(b.shape[1] for b in blocks)
    return pl.pallas_call(
        functools.partial(shared_kernel, kv_heads, n_blocks, tree is not None),
        out_shape=tuple(jax.ShapeDtypeStruct(s.shape, s.dtype) for s in state),
        grid_spec=pltpu.PrefetchScalarGridSpec(
            num_scalar_prefetch=1,
            grid=(1,),
            in_specs=[whole(a) for a in operands],
            out_specs=[whole(s) for s in state],
        ),
        compiler_params=pltpu.CompilerParams(vmem_limit_bytes=48 * 1024 * 1024),
        cost_estimate=pl.CostEstimate(
            flops=6 * kv_heads * rows * keys * HD,
            transcendentals=kv_heads * rows * keys,
            bytes_accessed=sum(b.size * 2 for b in blocks) + q.size * 2,
        ),
    )(flag, *operands)


def project_kernel(a_ref, w_ref, o_ref):
    o_ref[0] = jnp.dot(a_ref[...], w_ref[...], preferred_element_type=jnp.float32).astype(o_ref.dtype)


def project(attended, out_weight, owners):
    rows, depth = attended.shape
    columns = out_weight.shape[1] // owners
    return pl.pallas_call(
        project_kernel,
        out_shape=jax.ShapeDtypeStruct((owners, rows, columns), jnp.bfloat16),
        grid=(owners,),
        in_specs=[
            pl.BlockSpec((rows, depth), lambda c: (0, 0)),
            pl.BlockSpec((depth, columns), lambda c: (0, c)),
        ],
        out_specs=pl.BlockSpec((1, rows, columns), lambda c: (c, 0, 0)),
        cost_estimate=pl.CostEstimate(
            flops=2 * rows * depth * out_weight.shape[1],
            transcendentals=0,
            bytes_accessed=out_weight.size * 2 + attended.size * 2 + rows * out_weight.shape[1] * 2,
        ),
    )(attended, out_weight)


def tree_reach(parent_row):
    node_count = parent_row.shape[0]
    nodes = jnp.arange(node_count, dtype=jnp.int32)
    reach = jnp.eye(node_count, dtype=jnp.float32) + (parent_row[:, None] == nodes[None, :]).astype(
        jnp.float32
    )
    for _ in range(max(node_count - 1, 1).bit_length()):
        reach = jnp.minimum(jnp.dot(reach, reach, precision=lax.Precision.HIGHEST), 1.0)
    return reach > 0.5


def pick_group(shared_cache, group_ids, request):
    onehot = jnp.arange(group_ids.shape[0], dtype=jnp.int32) == request
    group = jnp.sum(jnp.where(onehot, group_ids, 0))
    picked = shared_cache[:, 0]
    for g in range(1, shared_cache.shape[1]):
        picked = jnp.where(group == g, shared_cache[:, g], picked)
    return picked


def partner(index, k, count):
    if count & (count - 1) == 0:
        return index ^ k
    return (index + k) % count


def exchange_shared(shared_cache, group_ids, req_index, req_count, distances):
    received = [pick_group(shared_cache, group_ids, req_index)]
    for k in distances:
        pairs = [(r, partner(r, k, req_count)) for r in range(req_count)]
        sent = pick_group(shared_cache, group_ids, partner(req_index, k, req_count))
        received.append(lax.ppermute(sent, "req", pairs))
    return received


def exchange_to_owner(shared_cache, group_ids, req_index, seq_index, req_count, seq_count, k):
    picked = pick_group(shared_cache, group_ids, partner(req_index, k, req_count))
    received = []
    for d in range(seq_count):
        head = partner(seq_index, d, seq_count)
        piece = lax.dynamic_slice_in_dim(picked, head * HD, HD, 2)
        pairs = [
            (r * seq_count + q, partner(r, k, req_count) * seq_count + partner(q, d, seq_count))
            for r in range(req_count)
            for q in range(seq_count)
        ]
        received.append(lax.ppermute(piece, ("req", "seq"), pairs))
    return received


def split16(x):
    high = lax.reduce_precision(x, exponent_bits=8, mantissa_bits=7)
    low = (x - high).astype(jnp.bfloat16)
    return high.astype(jnp.bfloat16), low


def join16(high, low):
    return high.astype(jnp.float32) + low.astype(jnp.float32)


def layer(
    draft_query,
    draft_kv,
    own_cache,
    shared_cache,
    out_weight,
    lengths,
    group_ids,
    parents,
    accepted,
):
    kv_heads = own_cache.shape[3] // HD
    draft_len = draft_query.shape[1]
    rows = QPK * draft_len
    seq_count = lax.axis_size("seq")
    seq_index = lax.axis_index("seq")
    req_index = lax.axis_index("req")
    req_count = lax.axis_size("req")
    cache_len = own_cache.shape[2]

    distances = list(range(1, req_count))
    owner_mode = kv_heads == seq_count and len(distances) > 0
    if owner_mode:
        owner_blocks = exchange_to_owner(
            shared_cache, group_ids, req_index, seq_index, req_count, seq_count, distances[-1]
        )
        distances = distances[:-1]
    blocks = exchange_shared(shared_cache, group_ids, req_index, req_count, distances)

    queries = (
        draft_query[0]
        .reshape(draft_len, kv_heads, QPK, HD)
        .transpose(1, 2, 0, 3)
        .reshape(kv_heads, rows, HD)
    )
    n_valid = jnp.clip(lengths[0] - seq_index * cache_len, 0, cache_len).astype(jnp.int32)
    state = own_attend(queries, own_cache[0], n_valid.reshape(1))

    reach = tree_reach(parents[0])
    reach_rows = jnp.tile(reach.astype(jnp.float32), (QPK, 1))
    flag = (seq_index == 0).astype(jnp.int32).reshape(1)
    state = shared_attend(queries, state, blocks[:2], (draft_kv[0], reach_rows, flag))
    for blk in blocks[2:]:
        state = shared_attend(queries, state, [blk])
    m, l, acc = state

    heads_dev = kv_heads * QPK
    share = heads_dev // seq_count
    part_out = (acc / l).astype(jnp.bfloat16).reshape(heads_dev, draft_len, HD)
    m_hi, m_lo = split16(m[..., 0].reshape(heads_dev, draft_len))
    l_hi, l_lo = split16(l[..., 0].reshape(heads_dev, draft_len))
    stats = jnp.stack(
        [jnp.concatenate([m_hi, m_lo], 1), jnp.concatenate([l_hi, l_lo], 1)], 1
    )
    packed = jnp.concatenate([part_out, stats], 1)
    packed = lax.all_to_all(packed, "seq", 0, 0, tiled=True)
    packed = packed.reshape(seq_count, share, draft_len + 2, 2 * draft_len)
    part_max = join16(packed[:, :, draft_len, :draft_len], packed[:, :, draft_len, draft_len:])
    part_total = join16(
        packed[:, :, draft_len + 1, :draft_len], packed[:, :, draft_len + 1, draft_len:]
    )
    part_sum = packed[:, :, :draft_len, :].astype(jnp.float32)
    final_max = jnp.max(part_max, axis=0)
    factor = jnp.exp2((part_max - final_max[None]) * EXP2_SCALE) * part_total
    final_total = jnp.sum(factor, axis=0)
    final_sum = jnp.sum(part_sum * factor[..., None], axis=0)
    if owner_mode:
        rows_owned = share * draft_len
        owned_query = lax.dynamic_index_in_dim(queries, seq_index, 0, keepdims=True)
        owned_state = (
            final_max.reshape(1, rows_owned, 1),
            jnp.broadcast_to(final_total.reshape(1, rows_owned, 1), (1, rows_owned, HD)),
            final_sum.reshape(1, rows_owned, HD),
        )
        _, owned_total, owned_sum = shared_attend(owned_query, owned_state, owner_blocks)
        attended = (owned_sum / owned_total).reshape(share, draft_len, HD).astype(jnp.bfloat16)
    else:
        attended = (final_sum / final_total[..., None]).astype(jnp.bfloat16)
    attended = jnp.transpose(attended, (1, 0, 2)).reshape(draft_len, share * HD)
    out_group = ("tensor", "seq")
    owners = lax.axis_size("tensor") * seq_count
    product = project(attended, out_weight, owners)
    pieces = lax.all_to_all(product, out_group, 0, 0, tiled=True)
    verified = jnp.sum(pieces.astype(jnp.float32), axis=0).astype(jnp.bfloat16)[None]
    accepted_kv = jnp.take(draft_kv[0], accepted[0], axis=1)[None]
    return (verified, accepted_kv)


def solution(mesh):
    placed = (
        P("req", None, "tensor"),
        P("req", None, None, "tensor"),
        P("req", None, "seq", "tensor"),
        P(None, None, ("req", "seq"), "tensor"),
        P(("tensor", "seq"), None),
        P("req"),
        P(),
        P("req", None),
        P("req", None),
    )
    return jax.shard_map(
        layer,
        mesh=mesh,
        in_specs=placed,
        out_specs=(P("req", None, ("tensor", "seq")), P("req", None, None, "tensor")),
        check_vma=False,
    )
```

```python
import functools

import jax
import jax.numpy as jnp
from jax import lax
from jax.experimental import pallas as pl
from jax.experimental.pallas import tpu as pltpu
from jax.sharding import PartitionSpec as P


HD = 128
QPK = 8
NEG_FILL = -1e30
SCALE = HD ** (-0.5)
EXP2_SCALE = SCALE * 1.4426950408889634
OWN_BLOCK = 2048


def step(m_prev, l_prev, acc_prev, q, k, v, ones, ok):
    scores = lax.dot_general(
        q, k, (((1,), (1,)), ((), ())), preferred_element_type=jnp.float32
    )
    if ok is not None:
        scores = jnp.where(ok, scores, NEG_FILL)
    m_new = jnp.maximum(m_prev, jnp.max(scores, axis=1, keepdims=True))
    alpha = jnp.exp2((m_prev - m_new) * EXP2_SCALE)
    weights = jnp.exp2((scores - m_new) * EXP2_SCALE)
    if ok is not None:
        weights = jnp.where(ok, weights, 0.0)
    weights = weights.astype(jnp.bfloat16)
    l_new = alpha * l_prev + jnp.dot(weights, ones, preferred_element_type=jnp.float32)
    acc_new = alpha * acc_prev + jnp.dot(weights, v, preferred_element_type=jnp.float32)
    return m_new, l_new, acc_new


def own_kernel(kv_heads, block, nv_ref, q_ref, kv_ref, ones_ref, m_out, l_out, acc_out, m_s, l_s, acc_s):
    j = pl.program_id(0)
    n_valid = nv_ref[0]

    @pl.when(j == 0)
    def _():
        m_s[...] = jnp.full(m_s.shape, NEG_FILL, jnp.float32)
        l_s[...] = jnp.zeros(l_s.shape, jnp.float32)
        acc_s[...] = jnp.zeros(acc_s.shape, jnp.float32)

    start = j * block

    def body(masked):
        ok = None
        if masked:
            cols = start + lax.broadcasted_iota(jnp.int32, (1, block), 1)
            ok = cols < n_valid

        def head(h, carry):
            cols_h = pl.ds(pl.multiple_of(h * HD, HD), HD)
            m, l, acc = step(
                m_s[h], l_s[h], acc_s[h], q_ref[h], kv_ref[0, :, cols_h], kv_ref[1, :, cols_h],
                ones_ref[...], ok,
            )
            m_s[h] = m
            l_s[h] = l
            acc_s[h] = acc
            return carry

        lax.fori_loop(0, kv_heads, head, 0)

    full = start + block <= n_valid
    part = jnp.logical_and(start < n_valid, jnp.logical_not(full))
    pl.when(full)(lambda: body(False))
    pl.when(part)(lambda: body(True))

    @pl.when(j == pl.num_programs(0) - 1)
    def _():
        m_out[...] = m_s[...]
        l_out[...] = l_s[...]
        acc_out[...] = acc_s[...]


def own_attend(q, kv, n_valid):
    kv_heads, rows, _ = q.shape
    cache_len = kv.shape[1]
    block = min(OWN_BLOCK, cache_len)
    n_blocks = cache_len // block

    def kv_map(j, nv):
        last = jnp.maximum((nv[0] + block - 1) // block - 1, 0)
        return (0, jnp.minimum(j, last), 0)

    state_shapes = (
        jax.ShapeDtypeStruct((kv_heads, rows, 1), jnp.float32),
        jax.ShapeDtypeStruct((kv_heads, rows, HD), jnp.float32),
        jax.ShapeDtypeStruct((kv_heads, rows, HD), jnp.float32),
    )
    ones = jnp.ones((block, HD), jnp.bfloat16)
    full3 = lambda j, nv: (0, 0, 0)
    return pl.pallas_call(
        functools.partial(own_kernel, kv_heads, block),
        out_shape=state_shapes,
        grid_spec=pltpu.PrefetchScalarGridSpec(
            num_scalar_prefetch=1,
            grid=(n_blocks,),
            in_specs=[
                pl.BlockSpec(q.shape, full3),
                pl.BlockSpec((2, block, kv.shape[2]), kv_map),
                pl.BlockSpec(ones.shape, lambda j, nv: (0, 0)),
            ],
            out_specs=[pl.BlockSpec(s.shape, full3) for s in state_shapes],
            scratch_shapes=[pltpu.VMEM(s.shape, jnp.float32) for s in state_shapes],
        ),
        compiler_params=pltpu.CompilerParams(dimension_semantics=("arbitrary",)),
        cost_estimate=pl.CostEstimate(
            flops=6 * kv_heads * rows * cache_len * HD,
            transcendentals=kv_heads * rows * cache_len,
            bytes_accessed=kv.size * 2 + q.size * 2,
        ),
    )(n_valid, q, kv, ones)


def shared_kernel(kv_heads, n_blocks, with_tree, flag_ref, q_ref, m_ref, l_ref, acc_ref, *rest):
    blocks = rest[:n_blocks]
    ones_ref = rest[n_blocks]
    rest = rest[n_blocks + 1:]
    if with_tree:
        dkv_ref, reach_ref, tree_ones_ref = rest[:3]
        rest = rest[3:]
    m_out, l_out, acc_out = rest[:3]

    def head(h, carry):
        cols_h = pl.ds(pl.multiple_of(h * HD, HD), HD)
        q = q_ref[h]
        m, l, acc = m_ref[h], l_ref[h], acc_ref[h]
        for blk in blocks:
            m, l, acc = step(
                m, l, acc, q, blk[0, :, cols_h], blk[1, :, cols_h], ones_ref[...], None
            )
        m_out[h] = m
        l_out[h] = l
        acc_out[h] = acc
        return carry

    lax.fori_loop(0, kv_heads, head, 0)

    if with_tree:
        @pl.when(flag_ref[0] == 1)
        def _():
            ok = reach_ref[...] > 0.5
            for h in range(kv_heads):
                cols_h = slice(h * HD, (h + 1) * HD)
                m, l, acc = step(
                    m_out[h], l_out[h], acc_out[h], q_ref[h],
                    dkv_ref[0, :, cols_h], dkv_ref[1, :, cols_h], tree_ones_ref[...], ok,
                )
                m_out[h] = m
                l_out[h] = l
                acc_out[h] = acc


def shared_attend(q, state, blocks, tree=None):
    kv_heads, rows, _ = q.shape
    n_blocks = len(blocks)
    whole = lambda a: pl.BlockSpec(a.shape, lambda i, f: (0,) * a.ndim)
    ones = jnp.ones((blocks[0].shape[1], HD), jnp.bfloat16)
    operands = (q,) + tuple(state) + tuple(blocks) + (ones,)
    if tree is not None:
        draft_kv, reach_rows, flag = tree
        operands += (draft_kv, reach_rows, jnp.ones((draft_kv.shape[1], HD), jnp.bfloat16))
    else:
        flag = jnp.zeros((1,), jnp.int32)
    keys = sum(b.shape[1] for b in blocks)
    return pl.pallas_call(
        functools.partial(shared_kernel, kv_heads, n_blocks, tree is not None),
        out_shape=tuple(jax.ShapeDtypeStruct(s.shape, s.dtype) for s in state),
        grid_spec=pltpu.PrefetchScalarGridSpec(
            num_scalar_prefetch=1,
            grid=(1,),
            in_specs=[whole(a) for a in operands],
            out_specs=[whole(s) for s in state],
        ),
        compiler_params=pltpu.CompilerParams(vmem_limit_bytes=48 * 1024 * 1024),
        cost_estimate=pl.CostEstimate(
            flops=6 * kv_heads * rows * keys * HD,
            transcendentals=kv_heads * rows * keys,
            bytes_accessed=sum(b.size * 2 for b in blocks) + q.size * 2,
        ),
    )(flag, *operands)


def tree_reach(parent_row):
    node_count = parent_row.shape[0]
    nodes = jnp.arange(node_count, dtype=jnp.int32)
    reach = jnp.eye(node_count, dtype=jnp.float32) + (parent_row[:, None] == nodes[None, :]).astype(
        jnp.float32
    )
    for _ in range(max(node_count - 1, 1).bit_length()):
        reach = jnp.minimum(jnp.dot(reach, reach, precision=lax.Precision.HIGHEST), 1.0)
    return reach > 0.5


def pick_group(shared_cache, group_ids, request):
    onehot = jnp.arange(group_ids.shape[0], dtype=jnp.int32) == request
    group = jnp.sum(jnp.where(onehot, group_ids, 0))
    picked = shared_cache[:, 0]
    for g in range(1, shared_cache.shape[1]):
        picked = jnp.where(group == g, shared_cache[:, g], picked)
    return picked


def partner(index, k, count):
    if count & (count - 1) == 0:
        return index ^ k
    return (index + k) % count


def exchange_shared(shared_cache, group_ids, req_index, req_count, distances):
    received = [pick_group(shared_cache, group_ids, req_index)]
    for k in distances:
        pairs = [(r, partner(r, k, req_count)) for r in range(req_count)]
        sent = pick_group(shared_cache, group_ids, partner(req_index, k, req_count))
        received.append(lax.ppermute(sent, "req", pairs))
    return received


def exchange_to_owner(shared_cache, group_ids, req_index, seq_index, req_count, seq_count, k):
    picked = pick_group(shared_cache, group_ids, partner(req_index, k, req_count))
    received = []
    for d in range(seq_count):
        head = partner(seq_index, d, seq_count)
        piece = lax.dynamic_slice_in_dim(picked, head * HD, HD, 2)
        pairs = [
            (r * seq_count + q, partner(r, k, req_count) * seq_count + partner(q, d, seq_count))
            for r in range(req_count)
            for q in range(seq_count)
        ]
        received.append(lax.ppermute(piece, ("req", "seq"), pairs))
    return received


def split16(x):
    high = lax.reduce_precision(x, exponent_bits=8, mantissa_bits=7)
    low = (x - high).astype(jnp.bfloat16)
    return high.astype(jnp.bfloat16), low


def join16(high, low):
    return high.astype(jnp.float32) + low.astype(jnp.float32)


def layer(
    draft_query,
    draft_kv,
    own_cache,
    shared_cache,
    out_weight,
    lengths,
    group_ids,
    parents,
    accepted,
):
    kv_heads = own_cache.shape[3] // HD
    draft_len = draft_query.shape[1]
    rows = QPK * draft_len
    seq_count = lax.axis_size("seq")
    seq_index = lax.axis_index("seq")
    req_index = lax.axis_index("req")
    req_count = lax.axis_size("req")
    cache_len = own_cache.shape[2]

    distances = list(range(1, req_count))
    owner_mode = kv_heads == seq_count and len(distances) > 0
    if owner_mode:
        owner_blocks = exchange_to_owner(
            shared_cache, group_ids, req_index, seq_index, req_count, seq_count, distances[-1]
        )
        distances = distances[:-1]
    blocks = exchange_shared(shared_cache, group_ids, req_index, req_count, distances)

    queries = (
        draft_query[0]
        .reshape(draft_len, kv_heads, QPK, HD)
        .transpose(1, 2, 0, 3)
        .reshape(kv_heads, rows, HD)
    )
    n_valid = jnp.clip(lengths[0] - seq_index * cache_len, 0, cache_len).astype(jnp.int32)
    state = own_attend(queries, own_cache[0], n_valid.reshape(1))

    reach = tree_reach(parents[0])
    reach_rows = jnp.tile(reach.astype(jnp.float32), (QPK, 1))
    flag = (seq_index == 0).astype(jnp.int32).reshape(1)
    state = shared_attend(queries, state, blocks[:2], (draft_kv[0], reach_rows, flag))
    for blk in blocks[2:]:
        state = shared_attend(queries, state, [blk])
    m, l, acc = state

    heads_dev = kv_heads * QPK
    share = heads_dev // seq_count
    part_out = (acc / l).astype(jnp.bfloat16).reshape(heads_dev, draft_len, HD)
    m_hi, m_lo = split16(m[..., 0].reshape(heads_dev, draft_len))
    l_hi, l_lo = split16(l[..., 0].reshape(heads_dev, draft_len))
    stats = jnp.stack(
        [jnp.concatenate([m_hi, m_lo], 1), jnp.concatenate([l_hi, l_lo], 1)], 1
    )
    packed = jnp.concatenate([part_out, stats], 1)
    packed = lax.all_to_all(packed, "seq", 0, 0, tiled=True)
    packed = packed.reshape(seq_count, share, draft_len + 2, 2 * draft_len)
    part_max = join16(packed[:, :, draft_len, :draft_len], packed[:, :, draft_len, draft_len:])
    part_total = join16(
        packed[:, :, draft_len + 1, :draft_len], packed[:, :, draft_len + 1, draft_len:]
    )
    part_sum = packed[:, :, :draft_len, :].astype(jnp.float32)
    final_max = jnp.max(part_max, axis=0)
    factor = jnp.exp2((part_max - final_max[None]) * EXP2_SCALE) * part_total
    final_total = jnp.sum(factor, axis=0)
    final_sum = jnp.sum(part_sum * factor[..., None], axis=0)
    if owner_mode:
        rows_owned = share * draft_len
        owned_query = lax.dynamic_index_in_dim(queries, seq_index, 0, keepdims=True)
        owned_state = (
            final_max.reshape(1, rows_owned, 1),
            jnp.broadcast_to(final_total.reshape(1, rows_owned, 1), (1, rows_owned, HD)),
            final_sum.reshape(1, rows_owned, HD),
        )
        _, owned_total, owned_sum = shared_attend(owned_query, owned_state, owner_blocks)
        attended = (owned_sum / owned_total).reshape(share, draft_len, HD).astype(jnp.bfloat16)
    else:
        attended = (final_sum / final_total[..., None]).astype(jnp.bfloat16)
    attended = jnp.transpose(attended, (1, 0, 2)).reshape(draft_len, share * HD)
    out_group = ("tensor", "seq")
    owners = lax.axis_size("tensor") * seq_count
    columns = out_weight.shape[1] // owners
    blocked = out_weight.reshape(out_weight.shape[0], owners, columns)
    half = columns // 2
    halves = []
    for lo in (0, half):
        product = jnp.einsum(
            "ik,kcj->cij",
            attended,
            blocked[:, :, lo:lo + half],
            preferred_element_type=jnp.float32,
        ).astype(jnp.bfloat16)
        pieces = lax.all_to_all(product, out_group, 0, 0, tiled=True)
        halves.append(jnp.sum(pieces.astype(jnp.float32), axis=0).astype(jnp.bfloat16))
    verified = jnp.concatenate(halves, 1)[None]
    accepted_kv = jnp.take(draft_kv[0], accepted[0], axis=1)[None]
    return (verified, accepted_kv)


def solution(mesh):
    placed = (
        P("req", None, "tensor"),
        P("req", None, None, "tensor"),
        P("req", None, "seq", "tensor"),
        P(None, None, ("req", "seq"), "tensor"),
        P(("tensor", "seq"), None),
        P("req"),
        P(),
        P("req", None),
        P("req", None),
    )
    return jax.shard_map(
        layer,
        mesh=mesh,
        in_specs=placed,
        out_specs=(P("req", None, ("tensor", "seq")), P("req", None, None, "tensor")),
        check_vma=False,
    )
```

```python
import functools

import jax
import jax.numpy as jnp
from jax import lax
from jax.experimental import pallas as pl
from jax.experimental.pallas import tpu as pltpu
from jax.sharding import PartitionSpec as P


HD = 128
QPK = 8
NEG_FILL = -1e30
SCALE = HD ** (-0.5)
EXP2_SCALE = SCALE * 1.4426950408889634
OWN_BLOCK = 2048


def step(m_prev, l_prev, acc_prev, q, k, v, ones, ok):
    scores = lax.dot_general(
        q, k, (((1,), (1,)), ((), ())), preferred_element_type=jnp.float32
    )
    if ok is not None:
        scores = jnp.where(ok, scores, NEG_FILL)
    m_new = jnp.maximum(m_prev, jnp.max(scores, axis=1, keepdims=True))
    alpha = jnp.exp2((m_prev - m_new) * EXP2_SCALE)
    weights = jnp.exp2((scores - m_new) * EXP2_SCALE)
    if ok is not None:
        weights = jnp.where(ok, weights, 0.0)
    weights = weights.astype(jnp.bfloat16)
    l_new = alpha * l_prev + jnp.dot(weights, ones, preferred_element_type=jnp.float32)
    acc_new = alpha * acc_prev + jnp.dot(weights, v, preferred_element_type=jnp.float32)
    return m_new, l_new, acc_new


def own_kernel(kv_heads, block, nv_ref, q_ref, kv_ref, ones_ref, m_out, l_out, acc_out, m_s, l_s, acc_s):
    j = pl.program_id(0)
    n_valid = nv_ref[0]

    @pl.when(j == 0)
    def _():
        m_s[...] = jnp.full(m_s.shape, NEG_FILL, jnp.float32)
        l_s[...] = jnp.zeros(l_s.shape, jnp.float32)
        acc_s[...] = jnp.zeros(acc_s.shape, jnp.float32)

    start = j * block

    def body(masked):
        ok = None
        if masked:
            cols = start + lax.broadcasted_iota(jnp.int32, (1, block), 1)
            ok = cols < n_valid

        def head(h, carry):
            cols_h = pl.ds(pl.multiple_of(h * HD, HD), HD)
            m, l, acc = step(
                m_s[h], l_s[h], acc_s[h], q_ref[h], kv_ref[0, :, cols_h], kv_ref[1, :, cols_h],
                ones_ref[...], ok,
            )
            m_s[h] = m
            l_s[h] = l
            acc_s[h] = acc
            return carry

        lax.fori_loop(0, kv_heads, head, 0)

    full = start + block <= n_valid
    part = jnp.logical_and(start < n_valid, jnp.logical_not(full))
    pl.when(full)(lambda: body(False))
    pl.when(part)(lambda: body(True))

    @pl.when(j == pl.num_programs(0) - 1)
    def _():
        m_out[...] = m_s[...]
        l_out[...] = l_s[...]
        acc_out[...] = acc_s[...]


def own_attend(q, kv, n_valid):
    kv_heads, rows, _ = q.shape
    cache_len = kv.shape[1]
    block = min(OWN_BLOCK, cache_len)
    n_blocks = cache_len // block

    def kv_map(j, nv):
        last = jnp.maximum((nv[0] + block - 1) // block - 1, 0)
        return (0, jnp.minimum(j, last), 0)

    state_shapes = (
        jax.ShapeDtypeStruct((kv_heads, rows, 1), jnp.float32),
        jax.ShapeDtypeStruct((kv_heads, rows, HD), jnp.float32),
        jax.ShapeDtypeStruct((kv_heads, rows, HD), jnp.float32),
    )
    ones = jnp.ones((block, HD), jnp.bfloat16)
    full3 = lambda j, nv: (0, 0, 0)
    return pl.pallas_call(
        functools.partial(own_kernel, kv_heads, block),
        out_shape=state_shapes,
        grid_spec=pltpu.PrefetchScalarGridSpec(
            num_scalar_prefetch=1,
            grid=(n_blocks,),
            in_specs=[
                pl.BlockSpec(q.shape, full3),
                pl.BlockSpec((2, block, kv.shape[2]), kv_map),
                pl.BlockSpec(ones.shape, lambda j, nv: (0, 0)),
            ],
            out_specs=[pl.BlockSpec(s.shape, full3) for s in state_shapes],
            scratch_shapes=[pltpu.VMEM(s.shape, jnp.float32) for s in state_shapes],
        ),
        compiler_params=pltpu.CompilerParams(dimension_semantics=("arbitrary",)),
        cost_estimate=pl.CostEstimate(
            flops=6 * kv_heads * rows * cache_len * HD,
            transcendentals=kv_heads * rows * cache_len,
            bytes_accessed=kv.size * 2 + q.size * 2,
        ),
    )(n_valid, q, kv, ones)


def shared_kernel(kv_heads, n_blocks, with_tree, flag_ref, q_ref, m_ref, l_ref, acc_ref, *rest):
    blocks = rest[:n_blocks]
    ones_ref = rest[n_blocks]
    rest = rest[n_blocks + 1:]
    if with_tree:
        dkv_ref, reach_ref, tree_ones_ref = rest[:3]
        rest = rest[3:]
    m_out, l_out, acc_out = rest[:3]

    def head(h, carry):
        cols_h = pl.ds(pl.multiple_of(h * HD, HD), HD)
        q = q_ref[h]
        m, l, acc = m_ref[h], l_ref[h], acc_ref[h]
        for blk in blocks:
            m, l, acc = step(
                m, l, acc, q, blk[0, :, cols_h], blk[1, :, cols_h], ones_ref[...], None
            )
        m_out[h] = m
        l_out[h] = l
        acc_out[h] = acc
        return carry

    lax.fori_loop(0, kv_heads, head, 0)

    if with_tree:
        @pl.when(flag_ref[0] == 1)
        def _():
            ok = reach_ref[...] > 0.5
            for h in range(kv_heads):
                cols_h = slice(h * HD, (h + 1) * HD)
                m, l, acc = step(
                    m_out[h], l_out[h], acc_out[h], q_ref[h],
                    dkv_ref[0, :, cols_h], dkv_ref[1, :, cols_h], tree_ones_ref[...], ok,
                )
                m_out[h] = m
                l_out[h] = l
                acc_out[h] = acc


def shared_attend(q, state, blocks, tree=None):
    kv_heads, rows, _ = q.shape
    n_blocks = len(blocks)
    whole = lambda a: pl.BlockSpec(a.shape, lambda i, f: (0,) * a.ndim)
    ones = jnp.ones((blocks[0].shape[1], HD), jnp.bfloat16)
    operands = (q,) + tuple(state) + tuple(blocks) + (ones,)
    if tree is not None:
        draft_kv, reach_rows, flag = tree
        operands += (draft_kv, reach_rows, jnp.ones((draft_kv.shape[1], HD), jnp.bfloat16))
    else:
        flag = jnp.zeros((1,), jnp.int32)
    keys = sum(b.shape[1] for b in blocks)
    return pl.pallas_call(
        functools.partial(shared_kernel, kv_heads, n_blocks, tree is not None),
        out_shape=tuple(jax.ShapeDtypeStruct(s.shape, s.dtype) for s in state),
        grid_spec=pltpu.PrefetchScalarGridSpec(
            num_scalar_prefetch=1,
            grid=(1,),
            in_specs=[whole(a) for a in operands],
            out_specs=[whole(s) for s in state],
        ),
        compiler_params=pltpu.CompilerParams(vmem_limit_bytes=48 * 1024 * 1024),
        cost_estimate=pl.CostEstimate(
            flops=6 * kv_heads * rows * keys * HD,
            transcendentals=kv_heads * rows * keys,
            bytes_accessed=sum(b.size * 2 for b in blocks) + q.size * 2,
        ),
    )(flag, *operands)


def tree_reach(parent_row):
    node_count = parent_row.shape[0]
    nodes = jnp.arange(node_count, dtype=jnp.int32)
    reach = jnp.eye(node_count, dtype=jnp.float32) + (parent_row[:, None] == nodes[None, :]).astype(
        jnp.float32
    )
    for _ in range(max(node_count - 1, 1).bit_length()):
        reach = jnp.minimum(jnp.dot(reach, reach, precision=lax.Precision.HIGHEST), 1.0)
    return reach > 0.5


def pick_group(shared_cache, group_ids, request):
    onehot = jnp.arange(group_ids.shape[0], dtype=jnp.int32) == request
    group = jnp.sum(jnp.where(onehot, group_ids, 0))
    picked = shared_cache[:, 0]
    for g in range(1, shared_cache.shape[1]):
        picked = jnp.where(group == g, shared_cache[:, g], picked)
    return picked


def partner(index, k, count):
    if count & (count - 1) == 0:
        return index ^ k
    return (index + k) % count


def exchange_shared(shared_cache, group_ids, req_index, req_count, distances):
    received = [pick_group(shared_cache, group_ids, req_index)]
    for k in distances:
        pairs = [(r, partner(r, k, req_count)) for r in range(req_count)]
        sent = pick_group(shared_cache, group_ids, partner(req_index, k, req_count))
        received.append(lax.ppermute(sent, "req", pairs))
    return received


def exchange_to_owner(shared_cache, group_ids, req_index, seq_index, req_count, seq_count, k):
    picked = pick_group(shared_cache, group_ids, partner(req_index, k, req_count))
    received = []
    for d in range(seq_count):
        head = partner(seq_index, d, seq_count)
        piece = lax.dynamic_slice_in_dim(picked, head * HD, HD, 2)
        pairs = [
            (r * seq_count + q, partner(r, k, req_count) * seq_count + partner(q, d, seq_count))
            for r in range(req_count)
            for q in range(seq_count)
        ]
        received.append(lax.ppermute(piece, ("req", "seq"), pairs))
    return received


def split16(x):
    high = lax.reduce_precision(x, exponent_bits=8, mantissa_bits=7)
    low = (x - high).astype(jnp.bfloat16)
    return high.astype(jnp.bfloat16), low


def join16(high, low):
    return high.astype(jnp.float32) + low.astype(jnp.float32)


def layer(
    draft_query,
    draft_kv,
    own_cache,
    shared_cache,
    out_weight,
    lengths,
    group_ids,
    parents,
    accepted,
):
    kv_heads = own_cache.shape[3] // HD
    draft_len = draft_query.shape[1]
    rows = QPK * draft_len
    seq_count = lax.axis_size("seq")
    seq_index = lax.axis_index("seq")
    req_index = lax.axis_index("req")
    req_count = lax.axis_size("req")
    cache_len = own_cache.shape[2]

    distances = list(range(1, req_count))
    owner_mode = kv_heads == seq_count and len(distances) > 0
    if owner_mode:
        owner_blocks = exchange_to_owner(
            shared_cache, group_ids, req_index, seq_index, req_count, seq_count, distances[-1]
        )
        distances = distances[:-1]
    blocks = exchange_shared(shared_cache, group_ids, req_index, req_count, distances)

    queries = (
        draft_query[0]
        .reshape(draft_len, kv_heads, QPK, HD)
        .transpose(1, 2, 0, 3)
        .reshape(kv_heads, rows, HD)
    )
    n_valid = jnp.clip(lengths[0] - seq_index * cache_len, 0, cache_len).astype(jnp.int32)
    state = own_attend(queries, own_cache[0], n_valid.reshape(1))

    reach = tree_reach(parents[0])
    reach_rows = jnp.tile(reach.astype(jnp.float32), (QPK, 1))
    flag = (seq_index == 0).astype(jnp.int32).reshape(1)
    state = shared_attend(queries, state, blocks[:2], (draft_kv[0], reach_rows, flag))
    for blk in blocks[2:]:
        state = shared_attend(queries, state, [blk])
    m, l, acc = state

    heads_dev = kv_heads * QPK
    share = heads_dev // seq_count
    part_out = (acc / l).astype(jnp.bfloat16).reshape(heads_dev, draft_len, HD)
    m_hi, m_lo = split16(m[..., 0].reshape(heads_dev, draft_len))
    l_hi, l_lo = split16(l[..., 0].reshape(heads_dev, draft_len))
    stats = jnp.stack(
        [jnp.concatenate([m_hi, m_lo], 1), jnp.concatenate([l_hi, l_lo], 1)], 1
    )
    packed = jnp.concatenate([part_out, stats], 1)
    packed = lax.all_to_all(packed, "seq", 0, 0, tiled=True)
    packed = packed.reshape(seq_count, share, draft_len + 2, 2 * draft_len)
    part_max = join16(packed[:, :, draft_len, :draft_len], packed[:, :, draft_len, draft_len:])
    part_total = join16(
        packed[:, :, draft_len + 1, :draft_len], packed[:, :, draft_len + 1, draft_len:]
    )
    part_sum = packed[:, :, :draft_len, :].astype(jnp.float32)
    final_max = jnp.max(part_max, axis=0)
    factor = jnp.exp2((part_max - final_max[None]) * EXP2_SCALE) * part_total
    final_total = jnp.sum(factor, axis=0)
    final_sum = jnp.sum(part_sum * factor[..., None], axis=0)
    if owner_mode:
        rows_owned = share * draft_len
        owned_query = lax.dynamic_index_in_dim(queries, seq_index, 0, keepdims=True)
        owned_state = (
            final_max.reshape(1, rows_owned, 1),
            jnp.broadcast_to(final_total.reshape(1, rows_owned, 1), (1, rows_owned, HD)),
            final_sum.reshape(1, rows_owned, HD),
        )
        _, owned_total, owned_sum = shared_attend(owned_query, owned_state, owner_blocks)
        attended = (owned_sum / owned_total).reshape(share, draft_len, HD).astype(jnp.bfloat16)
    else:
        attended = (final_sum / final_total[..., None]).astype(jnp.bfloat16)
    attended = jnp.transpose(attended, (1, 0, 2)).reshape(draft_len, share * HD)
    out_group = ("tensor", "seq")
    owners = lax.axis_size("tensor") * seq_count
    columns = out_weight.shape[1] // owners
    product = jnp.einsum(
        "ik,kcj->cij",
        attended,
        out_weight.reshape(out_weight.shape[0], owners, columns),
        preferred_element_type=jnp.float32,
    ).astype(jnp.bfloat16)
    pieces = lax.all_to_all(product, out_group, 0, 0, tiled=True)
    verified = jnp.sum(pieces.astype(jnp.float32), axis=0).astype(jnp.bfloat16)[None]
    accepted_kv = jnp.take(draft_kv[0], accepted[0], axis=1)[None]
    return (verified, accepted_kv)


def solution(mesh):
    placed = (
        P("req", None, "tensor"),
        P("req", None, None, "tensor"),
        P("req", None, "seq", "tensor"),
        P(None, None, ("req", "seq"), "tensor"),
        P(("tensor", "seq"), None),
        P("req"),
        P(),
        P("req", None),
        P("req", None),
    )
    return jax.shard_map(
        layer,
        mesh=mesh,
        in_specs=placed,
        out_specs=(P("req", None, ("tensor", "seq")), P("req", None, None, "tensor")),
        check_vma=False,
    )
```

```python
import functools

import jax
import jax.numpy as jnp
from jax import lax
from jax.experimental import pallas as pl
from jax.experimental.pallas import tpu as pltpu
from jax.sharding import PartitionSpec as P


HD = 128
QPK = 8
NEG_FILL = -1e30
SCALE = HD ** (-0.5)
EXP2_SCALE = SCALE * 1.4426950408889634
OWN_BLOCK = 2048


def step(m_prev, l_prev, acc_prev, q, k, v, ones, ok):
    scores = lax.dot_general(
        q, k, (((1,), (1,)), ((), ())), preferred_element_type=jnp.float32
    )
    if ok is not None:
        scores = jnp.where(ok, scores, NEG_FILL)
    m_new = jnp.maximum(m_prev, jnp.max(scores, axis=1, keepdims=True))
    alpha = jnp.exp2((m_prev - m_new) * EXP2_SCALE)
    weights = jnp.exp2((scores - m_new) * EXP2_SCALE)
    if ok is not None:
        weights = jnp.where(ok, weights, 0.0)
    weights = weights.astype(jnp.bfloat16)
    l_new = alpha * l_prev + jnp.dot(weights, ones, preferred_element_type=jnp.float32)
    acc_new = alpha * acc_prev + jnp.dot(weights, v, preferred_element_type=jnp.float32)
    return m_new, l_new, acc_new


def own_kernel(kv_heads, block, nv_ref, q_ref, kv_ref, ones_ref, m_out, l_out, acc_out, m_s, l_s, acc_s):
    j = pl.program_id(0)
    n_valid = nv_ref[0]

    @pl.when(j == 0)
    def _():
        m_s[...] = jnp.full(m_s.shape, NEG_FILL, jnp.float32)
        l_s[...] = jnp.zeros(l_s.shape, jnp.float32)
        acc_s[...] = jnp.zeros(acc_s.shape, jnp.float32)

    start = j * block

    def body(masked):
        ok = None
        if masked:
            cols = start + lax.broadcasted_iota(jnp.int32, (1, block), 1)
            ok = cols < n_valid

        def head(h, carry):
            cols_h = pl.ds(pl.multiple_of(h * HD, HD), HD)
            m, l, acc = step(
                m_s[h], l_s[h], acc_s[h], q_ref[h], kv_ref[0, :, cols_h], kv_ref[1, :, cols_h],
                ones_ref[...], ok,
            )
            m_s[h] = m
            l_s[h] = l
            acc_s[h] = acc
            return carry

        lax.fori_loop(0, kv_heads, head, 0)

    full = start + block <= n_valid
    part = jnp.logical_and(start < n_valid, jnp.logical_not(full))
    pl.when(full)(lambda: body(False))
    pl.when(part)(lambda: body(True))

    @pl.when(j == pl.num_programs(0) - 1)
    def _():
        m_out[...] = m_s[...]
        l_out[...] = l_s[...]
        acc_out[...] = acc_s[...]


def own_attend(q, kv, n_valid):
    kv_heads, rows, _ = q.shape
    cache_len = kv.shape[1]
    block = min(OWN_BLOCK, cache_len)
    n_blocks = cache_len // block

    def kv_map(j, nv):
        last = jnp.maximum((nv[0] + block - 1) // block - 1, 0)
        return (0, jnp.minimum(j, last), 0)

    state_shapes = (
        jax.ShapeDtypeStruct((kv_heads, rows, 1), jnp.float32),
        jax.ShapeDtypeStruct((kv_heads, rows, HD), jnp.float32),
        jax.ShapeDtypeStruct((kv_heads, rows, HD), jnp.float32),
    )
    ones = jnp.ones((block, HD), jnp.bfloat16)
    full3 = lambda j, nv: (0, 0, 0)
    return pl.pallas_call(
        functools.partial(own_kernel, kv_heads, block),
        out_shape=state_shapes,
        grid_spec=pltpu.PrefetchScalarGridSpec(
            num_scalar_prefetch=1,
            grid=(n_blocks,),
            in_specs=[
                pl.BlockSpec(q.shape, full3),
                pl.BlockSpec((2, block, kv.shape[2]), kv_map),
                pl.BlockSpec(ones.shape, lambda j, nv: (0, 0)),
            ],
            out_specs=[pl.BlockSpec(s.shape, full3) for s in state_shapes],
            scratch_shapes=[pltpu.VMEM(s.shape, jnp.float32) for s in state_shapes],
        ),
        compiler_params=pltpu.CompilerParams(dimension_semantics=("arbitrary",)),
        cost_estimate=pl.CostEstimate(
            flops=6 * kv_heads * rows * cache_len * HD,
            transcendentals=kv_heads * rows * cache_len,
            bytes_accessed=kv.size * 2 + q.size * 2,
        ),
    )(n_valid, q, kv, ones)


def shared_kernel(kv_heads, n_blocks, with_tree, flag_ref, q_ref, m_ref, l_ref, acc_ref, *rest):
    blocks = rest[:n_blocks]
    ones_ref = rest[n_blocks]
    rest = rest[n_blocks + 1:]
    if with_tree:
        dkv_ref, reach_ref, tree_ones_ref = rest[:3]
        rest = rest[3:]
    m_out, l_out, acc_out = rest[:3]

    def head(h, carry):
        cols_h = pl.ds(pl.multiple_of(h * HD, HD), HD)
        q = q_ref[h]
        m, l, acc = m_ref[h], l_ref[h], acc_ref[h]
        for blk in blocks:
            m, l, acc = step(
                m, l, acc, q, blk[0, :, cols_h], blk[1, :, cols_h], ones_ref[...], None
            )
        m_out[h] = m
        l_out[h] = l
        acc_out[h] = acc
        return carry

    lax.fori_loop(0, kv_heads, head, 0)

    if with_tree:
        @pl.when(flag_ref[0] == 1)
        def _():
            ok = reach_ref[...] > 0.5
            for h in range(kv_heads):
                cols_h = slice(h * HD, (h + 1) * HD)
                m, l, acc = step(
                    m_out[h], l_out[h], acc_out[h], q_ref[h],
                    dkv_ref[0, :, cols_h], dkv_ref[1, :, cols_h], tree_ones_ref[...], ok,
                )
                m_out[h] = m
                l_out[h] = l
                acc_out[h] = acc


def shared_attend(q, state, blocks, tree=None, local=None):
    kv_heads, rows, _ = q.shape
    whole = lambda a: pl.BlockSpec(a.shape, lambda i, f: (0,) * a.ndim)
    blocks = tuple(blocks)
    block_specs = [whole(b) for b in blocks]
    group = jnp.zeros((1,), jnp.int32)
    if local is not None:
        cache, group = local
        picked = pl.BlockSpec(
            (cache.shape[0], None) + cache.shape[2:], lambda i, f: (0, f[1], 0, 0)
        )
        blocks = (cache,) + blocks
        block_specs = [picked] + block_specs
    n_blocks = len(blocks)
    block_len = blocks[-1].shape[-2]
    ones = jnp.ones((block_len, HD), jnp.bfloat16)
    operands = (q,) + tuple(state) + blocks + (ones,)
    specs = [whole(a) for a in (q,) + tuple(state)] + block_specs + [whole(ones)]
    if tree is not None:
        draft_kv, reach_rows, flag = tree
        extra = (draft_kv, reach_rows, jnp.ones((draft_kv.shape[1], HD), jnp.bfloat16))
        operands += extra
        specs += [whole(a) for a in extra]
    else:
        flag = jnp.zeros((1,), jnp.int32)
    keys = block_len * n_blocks
    scalars = jnp.concatenate([flag.reshape(1), group.reshape(1)]).astype(jnp.int32)
    return pl.pallas_call(
        functools.partial(shared_kernel, kv_heads, n_blocks, tree is not None),
        out_shape=tuple(jax.ShapeDtypeStruct(s.shape, s.dtype) for s in state),
        grid_spec=pltpu.PrefetchScalarGridSpec(
            num_scalar_prefetch=1,
            grid=(1,),
            in_specs=specs,
            out_specs=[whole(s) for s in state],
        ),
        compiler_params=pltpu.CompilerParams(vmem_limit_bytes=48 * 1024 * 1024),
        cost_estimate=pl.CostEstimate(
            flops=6 * kv_heads * rows * keys * HD,
            transcendentals=kv_heads * rows * keys,
            bytes_accessed=keys * blocks[-1].shape[-1] * 4 + q.size * 2,
        ),
    )(scalars, *operands)


def tree_reach(parent_row):
    node_count = parent_row.shape[0]
    nodes = jnp.arange(node_count, dtype=jnp.int32)
    reach = jnp.eye(node_count, dtype=jnp.float32) + (parent_row[:, None] == nodes[None, :]).astype(
        jnp.float32
    )
    for _ in range(max(node_count - 1, 1).bit_length()):
        reach = jnp.minimum(jnp.dot(reach, reach, precision=lax.Precision.HIGHEST), 1.0)
    return reach > 0.5


def pick_group(shared_cache, group_ids, request):
    onehot = jnp.arange(group_ids.shape[0], dtype=jnp.int32) == request
    group = jnp.sum(jnp.where(onehot, group_ids, 0))
    picked = shared_cache[:, 0]
    for g in range(1, shared_cache.shape[1]):
        picked = jnp.where(group == g, shared_cache[:, g], picked)
    return picked


def partner(index, k, count):
    if count & (count - 1) == 0:
        return index ^ k
    return (index + k) % count


def exchange_shared(shared_cache, group_ids, req_index, req_count, distances):
    received = []
    for k in distances:
        pairs = [(r, partner(r, k, req_count)) for r in range(req_count)]
        sent = pick_group(shared_cache, group_ids, partner(req_index, k, req_count))
        received.append(lax.ppermute(sent, "req", pairs))
    return received


def exchange_to_owner(shared_cache, group_ids, req_index, seq_index, req_count, seq_count, k):
    picked = pick_group(shared_cache, group_ids, partner(req_index, k, req_count))
    received = []
    for d in range(seq_count):
        head = partner(seq_index, d, seq_count)
        piece = lax.dynamic_slice_in_dim(picked, head * HD, HD, 2)
        pairs = [
            (r * seq_count + q, partner(r, k, req_count) * seq_count + partner(q, d, seq_count))
            for r in range(req_count)
            for q in range(seq_count)
        ]
        received.append(lax.ppermute(piece, ("req", "seq"), pairs))
    return received


def split16(x):
    high = lax.reduce_precision(x, exponent_bits=8, mantissa_bits=7)
    low = (x - high).astype(jnp.bfloat16)
    return high.astype(jnp.bfloat16), low


def join16(high, low):
    return high.astype(jnp.float32) + low.astype(jnp.float32)


def layer(
    draft_query,
    draft_kv,
    own_cache,
    shared_cache,
    out_weight,
    lengths,
    group_ids,
    parents,
    accepted,
):
    kv_heads = own_cache.shape[3] // HD
    draft_len = draft_query.shape[1]
    rows = QPK * draft_len
    seq_count = lax.axis_size("seq")
    seq_index = lax.axis_index("seq")
    req_index = lax.axis_index("req")
    req_count = lax.axis_size("req")
    cache_len = own_cache.shape[2]

    distances = list(range(1, req_count))
    owner_mode = kv_heads == seq_count and len(distances) > 0
    if owner_mode:
        owner_blocks = exchange_to_owner(
            shared_cache, group_ids, req_index, seq_index, req_count, seq_count, distances[-1]
        )
        distances = distances[:-1]
    blocks = exchange_shared(shared_cache, group_ids, req_index, req_count, distances)

    queries = (
        draft_query[0]
        .reshape(draft_len, kv_heads, QPK, HD)
        .transpose(1, 2, 0, 3)
        .reshape(kv_heads, rows, HD)
    )
    n_valid = jnp.clip(lengths[0] - seq_index * cache_len, 0, cache_len).astype(jnp.int32)
    state = own_attend(queries, own_cache[0], n_valid.reshape(1))

    reach = tree_reach(parents[0])
    reach_rows = jnp.tile(reach.astype(jnp.float32), (QPK, 1))
    flag = (seq_index == 0).astype(jnp.int32).reshape(1)
    own_group = jnp.sum(
        jnp.where(jnp.arange(group_ids.shape[0], dtype=jnp.int32) == req_index, group_ids, 0)
    )
    state = shared_attend(
        queries, state, blocks[:1], (draft_kv[0], reach_rows, flag), (shared_cache, own_group)
    )
    for blk in blocks[1:]:
        state = shared_attend(queries, state, [blk])
    m, l, acc = state

    heads_dev = kv_heads * QPK
    share = heads_dev // seq_count
    part_out = (acc / l).astype(jnp.bfloat16).reshape(heads_dev, draft_len, HD)
    m_hi, m_lo = split16(m[..., 0].reshape(heads_dev, draft_len))
    l_hi, l_lo = split16(l[..., 0].reshape(heads_dev, draft_len))
    stats = jnp.stack(
        [jnp.concatenate([m_hi, m_lo], 1), jnp.concatenate([l_hi, l_lo], 1)], 1
    )
    packed = jnp.concatenate([part_out, stats], 1)
    packed = lax.all_to_all(packed, "seq", 0, 0, tiled=True)
    packed = packed.reshape(seq_count, share, draft_len + 2, 2 * draft_len)
    part_max = join16(packed[:, :, draft_len, :draft_len], packed[:, :, draft_len, draft_len:])
    part_total = join16(
        packed[:, :, draft_len + 1, :draft_len], packed[:, :, draft_len + 1, draft_len:]
    )
    part_sum = packed[:, :, :draft_len, :].astype(jnp.float32)
    final_max = jnp.max(part_max, axis=0)
    factor = jnp.exp2((part_max - final_max[None]) * EXP2_SCALE) * part_total
    final_total = jnp.sum(factor, axis=0)
    final_sum = jnp.sum(part_sum * factor[..., None], axis=0)
    if owner_mode:
        rows_owned = share * draft_len
        owned_query = lax.dynamic_index_in_dim(queries, seq_index, 0, keepdims=True)
        owned_state = (
            final_max.reshape(1, rows_owned, 1),
            jnp.broadcast_to(final_total.reshape(1, rows_owned, 1), (1, rows_owned, HD)),
            final_sum.reshape(1, rows_owned, HD),
        )
        _, owned_total, owned_sum = shared_attend(owned_query, owned_state, owner_blocks)
        attended = (owned_sum / owned_total).reshape(share, draft_len, HD).astype(jnp.bfloat16)
    else:
        attended = (final_sum / final_total[..., None]).astype(jnp.bfloat16)
    attended = jnp.transpose(attended, (1, 0, 2)).reshape(draft_len, share * HD)
    out_group = ("tensor", "seq")
    owners = lax.axis_size("tensor") * seq_count
    columns = out_weight.shape[1] // owners
    product = jnp.einsum(
        "ik,kcj->cij",
        attended,
        out_weight.reshape(out_weight.shape[0], owners, columns),
        preferred_element_type=jnp.float32,
    ).astype(jnp.bfloat16)
    pieces = lax.all_to_all(product, out_group, 0, 0, tiled=True)
    verified = jnp.sum(pieces.astype(jnp.float32), axis=0).astype(jnp.bfloat16)[None]
    accepted_kv = jnp.take(draft_kv[0], accepted[0], axis=1)[None]
    return (verified, accepted_kv)


def solution(mesh):
    placed = (
        P("req", None, "tensor"),
        P("req", None, None, "tensor"),
        P("req", None, "seq", "tensor"),
        P(None, None, ("req", "seq"), "tensor"),
        P(("tensor", "seq"), None),
        P("req"),
        P(),
        P("req", None),
        P("req", None),
    )
    return jax.shard_map(
        layer,
        mesh=mesh,
        in_specs=placed,
        out_specs=(P("req", None, ("tensor", "seq")), P("req", None, None, "tensor")),
        check_vma=False,
    )
```

```python
import functools

import jax
import jax.numpy as jnp
from jax import lax
from jax.experimental import pallas as pl
from jax.experimental.pallas import tpu as pltpu
from jax.sharding import PartitionSpec as P


HD = 128
QPK = 8
NEG_FILL = -1e30
SCALE = HD ** (-0.5)
EXP2_SCALE = SCALE * 1.4426950408889634
OWN_BLOCK = 2048


def step(m_prev, l_prev, acc_prev, q, k, v, ones, ok):
    scores = lax.dot_general(
        q, k, (((1,), (1,)), ((), ())), preferred_element_type=jnp.float32
    )
    if ok is not None:
        scores = jnp.where(ok, scores, NEG_FILL)
    m_new = jnp.maximum(m_prev, jnp.max(scores, axis=1, keepdims=True))
    alpha = jnp.exp2((m_prev - m_new) * EXP2_SCALE)
    weights = jnp.exp2((scores - m_new) * EXP2_SCALE)
    if ok is not None:
        weights = jnp.where(ok, weights, 0.0)
    weights = weights.astype(jnp.bfloat16)
    l_new = alpha * l_prev + jnp.dot(weights, ones, preferred_element_type=jnp.float32)
    acc_new = alpha * acc_prev + jnp.dot(weights, v, preferred_element_type=jnp.float32)
    return m_new, l_new, acc_new


def own_kernel(kv_heads, block, nv_ref, q_ref, kv_ref, ones_ref, m_out, l_out, acc_out, m_s, l_s, acc_s):
    j = pl.program_id(0)
    n_valid = nv_ref[0]

    @pl.when(j == 0)
    def _():
        m_s[...] = jnp.full(m_s.shape, NEG_FILL, jnp.float32)
        l_s[...] = jnp.zeros(l_s.shape, jnp.float32)
        acc_s[...] = jnp.zeros(acc_s.shape, jnp.float32)

    start = j * block

    def body(masked):
        ok = None
        if masked:
            cols = start + lax.broadcasted_iota(jnp.int32, (1, block), 1)
            ok = cols < n_valid

        def head(h, carry):
            cols_h = pl.ds(pl.multiple_of(h * HD, HD), HD)
            m, l, acc = step(
                m_s[h], l_s[h], acc_s[h], q_ref[h], kv_ref[0, :, cols_h], kv_ref[1, :, cols_h],
                ones_ref[...], ok,
            )
            m_s[h] = m
            l_s[h] = l
            acc_s[h] = acc
            return carry

        lax.fori_loop(0, kv_heads, head, 0)

    full = start + block <= n_valid
    part = jnp.logical_and(start < n_valid, jnp.logical_not(full))
    pl.when(full)(lambda: body(False))
    pl.when(part)(lambda: body(True))

    @pl.when(j == pl.num_programs(0) - 1)
    def _():
        m_out[...] = m_s[...]
        l_out[...] = l_s[...]
        acc_out[...] = acc_s[...]


def own_attend(q, kv, n_valid):
    kv_heads, rows, _ = q.shape
    cache_len = kv.shape[1]
    block = min(OWN_BLOCK, cache_len)
    n_blocks = cache_len // block

    def kv_map(j, nv):
        last = jnp.maximum((nv[0] + block - 1) // block - 1, 0)
        return (0, jnp.minimum(j, last), 0)

    state_shapes = (
        jax.ShapeDtypeStruct((kv_heads, rows, 1), jnp.float32),
        jax.ShapeDtypeStruct((kv_heads, rows, HD), jnp.float32),
        jax.ShapeDtypeStruct((kv_heads, rows, HD), jnp.float32),
    )
    ones = jnp.ones((block, HD), jnp.bfloat16)
    full3 = lambda j, nv: (0, 0, 0)
    return pl.pallas_call(
        functools.partial(own_kernel, kv_heads, block),
        out_shape=state_shapes,
        grid_spec=pltpu.PrefetchScalarGridSpec(
            num_scalar_prefetch=1,
            grid=(n_blocks,),
            in_specs=[
                pl.BlockSpec(q.shape, full3),
                pl.BlockSpec((2, block, kv.shape[2]), kv_map),
                pl.BlockSpec(ones.shape, lambda j, nv: (0, 0)),
            ],
            out_specs=[pl.BlockSpec(s.shape, full3) for s in state_shapes],
            scratch_shapes=[pltpu.VMEM(s.shape, jnp.float32) for s in state_shapes],
        ),
        compiler_params=pltpu.CompilerParams(dimension_semantics=("arbitrary",)),
        cost_estimate=pl.CostEstimate(
            flops=6 * kv_heads * rows * cache_len * HD,
            transcendentals=kv_heads * rows * cache_len,
            bytes_accessed=kv.size * 2 + q.size * 2,
        ),
    )(n_valid, q, kv, ones)


def shared_kernel(kv_heads, n_blocks, with_tree, flag_ref, q_ref, m_ref, l_ref, acc_ref, *rest):
    blocks = rest[:n_blocks]
    ones_ref = rest[n_blocks]
    rest = rest[n_blocks + 1:]
    if with_tree:
        dkv_ref, reach_ref, tree_ones_ref = rest[:3]
        rest = rest[3:]
    m_out, l_out, acc_out = rest[:3]

    def head(h, carry):
        cols_h = pl.ds(pl.multiple_of(h * HD, HD), HD)
        q = q_ref[h]
        m, l, acc = m_ref[h], l_ref[h], acc_ref[h]
        for blk in blocks:
            m, l, acc = step(
                m, l, acc, q, blk[0, :, cols_h], blk[1, :, cols_h], ones_ref[...], None
            )
        m_out[h] = m
        l_out[h] = l
        acc_out[h] = acc
        return carry

    lax.fori_loop(0, kv_heads, head, 0)

    if with_tree:
        @pl.when(flag_ref[0] == 1)
        def _():
            ok = reach_ref[...] > 0.5
            for h in range(kv_heads):
                cols_h = slice(h * HD, (h + 1) * HD)
                m, l, acc = step(
                    m_out[h], l_out[h], acc_out[h], q_ref[h],
                    dkv_ref[0, :, cols_h], dkv_ref[1, :, cols_h], tree_ones_ref[...], ok,
                )
                m_out[h] = m
                l_out[h] = l
                acc_out[h] = acc


def shared_attend(q, state, blocks, tree=None, local=None):
    kv_heads, rows, _ = q.shape
    whole = lambda a: pl.BlockSpec(a.shape, lambda i, f: (0,) * a.ndim)
    blocks = tuple(blocks)
    block_specs = [whole(b) for b in blocks]
    group = jnp.zeros((1,), jnp.int32)
    if local is not None:
        cache, group = local
        picked = pl.BlockSpec(
            (cache.shape[0], None) + cache.shape[2:], lambda i, f: (0, f[1], 0, 0)
        )
        blocks = (cache,) + blocks
        block_specs = [picked] + block_specs
    n_blocks = len(blocks)
    block_len = blocks[-1].shape[-2]
    ones = jnp.ones((block_len, HD), jnp.bfloat16)
    operands = (q,) + tuple(state) + blocks + (ones,)
    specs = [whole(a) for a in (q,) + tuple(state)] + block_specs + [whole(ones)]
    if tree is not None:
        draft_kv, reach_rows, flag = tree
        extra = (draft_kv, reach_rows, jnp.ones((draft_kv.shape[1], HD), jnp.bfloat16))
        operands += extra
        specs += [whole(a) for a in extra]
    else:
        flag = jnp.zeros((1,), jnp.int32)
    keys = block_len * n_blocks
    scalars = jnp.concatenate([flag.reshape(1), group.reshape(1)]).astype(jnp.int32)
    return pl.pallas_call(
        functools.partial(shared_kernel, kv_heads, n_blocks, tree is not None),
        out_shape=tuple(jax.ShapeDtypeStruct(s.shape, s.dtype) for s in state),
        grid_spec=pltpu.PrefetchScalarGridSpec(
            num_scalar_prefetch=1,
            grid=(1,),
            in_specs=specs,
            out_specs=[whole(s) for s in state],
        ),
        compiler_params=pltpu.CompilerParams(vmem_limit_bytes=48 * 1024 * 1024),
        cost_estimate=pl.CostEstimate(
            flops=6 * kv_heads * rows * keys * HD,
            transcendentals=kv_heads * rows * keys,
            bytes_accessed=keys * blocks[-1].shape[-1] * 4 + q.size * 2,
        ),
    )(scalars, *operands)


def tree_reach(parent_row):
    node_count = parent_row.shape[0]
    nodes = jnp.arange(node_count, dtype=jnp.int32)
    reach = jnp.eye(node_count, dtype=jnp.float32) + (parent_row[:, None] == nodes[None, :]).astype(
        jnp.float32
    )
    for _ in range(max(node_count - 1, 1).bit_length()):
        reach = jnp.minimum(jnp.dot(reach, reach, precision=lax.Precision.HIGHEST), 1.0)
    return reach > 0.5


def pick_group(shared_cache, group_ids, request):
    onehot = jnp.arange(group_ids.shape[0], dtype=jnp.int32) == request
    group = jnp.sum(jnp.where(onehot, group_ids, 0))
    picked = shared_cache[:, 0]
    for g in range(1, shared_cache.shape[1]):
        picked = jnp.where(group == g, shared_cache[:, g], picked)
    return picked


def partner(index, k, count):
    if count & (count - 1) == 0:
        return index ^ k
    return (index + k) % count


def exchange_shared(shared_cache, group_ids, req_index, req_count, distances):
    received = []
    for k in distances:
        pairs = [(r, partner(r, k, req_count)) for r in range(req_count)]
        sent = pick_group(shared_cache, group_ids, partner(req_index, k, req_count))
        received.append(lax.ppermute(sent, "req", pairs))
    return received


def exchange_to_owner(shared_cache, group_ids, req_index, seq_index, req_count, seq_count, k):
    picked = pick_group(shared_cache, group_ids, partner(req_index, k, req_count))
    received = []
    for d in range(seq_count):
        head = partner(seq_index, d, seq_count)
        piece = lax.dynamic_slice_in_dim(picked, head * HD, HD, 2)
        pairs = [
            (r * seq_count + q, partner(r, k, req_count) * seq_count + partner(q, d, seq_count))
            for r in range(req_count)
            for q in range(seq_count)
        ]
        received.append(lax.ppermute(piece, ("req", "seq"), pairs))
    return received


def split16(x):
    high = lax.reduce_precision(x, exponent_bits=8, mantissa_bits=7)
    low = (x - high).astype(jnp.bfloat16)
    return high.astype(jnp.bfloat16), low


def join16(high, low):
    return high.astype(jnp.float32) + low.astype(jnp.float32)


def layer(
    draft_query,
    draft_kv,
    own_cache,
    shared_cache,
    out_weight,
    lengths,
    group_ids,
    parents,
    accepted,
):
    kv_heads = own_cache.shape[3] // HD
    draft_len = draft_query.shape[1]
    rows = QPK * draft_len
    seq_count = lax.axis_size("seq")
    seq_index = lax.axis_index("seq")
    req_index = lax.axis_index("req")
    req_count = lax.axis_size("req")
    cache_len = own_cache.shape[2]

    distances = list(range(1, req_count))
    owner_mode = kv_heads == seq_count and len(distances) > 0
    if owner_mode:
        owner_blocks = exchange_to_owner(
            shared_cache, group_ids, req_index, seq_index, req_count, seq_count, distances[-1]
        )
        distances = distances[:-1]
    blocks = exchange_shared(shared_cache, group_ids, req_index, req_count, distances)

    queries = (
        draft_query[0]
        .reshape(draft_len, kv_heads, QPK, HD)
        .transpose(1, 2, 0, 3)
        .reshape(kv_heads, rows, HD)
    )
    n_valid = jnp.clip(lengths[0] - seq_index * cache_len, 0, cache_len).astype(jnp.int32)
    state = own_attend(queries, own_cache[0], n_valid.reshape(1))

    reach = tree_reach(parents[0])
    reach_rows = jnp.tile(reach.astype(jnp.float32), (QPK, 1))
    flag = (seq_index == 0).astype(jnp.int32).reshape(1)
    own_group = jnp.sum(
        jnp.where(jnp.arange(group_ids.shape[0], dtype=jnp.int32) == req_index, group_ids, 0)
    )
    state = shared_attend(
        queries, state, blocks[:1], (draft_kv[0], reach_rows, flag), (shared_cache, own_group)
    )
    for blk in blocks[1:]:
        state = shared_attend(queries, state, [blk])
    m, l, acc = state

    heads_dev = kv_heads * QPK
    share = heads_dev // seq_count
    part_out = (acc / l).astype(jnp.bfloat16).reshape(heads_dev, draft_len, HD)
    m_hi, m_lo = split16(m[..., 0].reshape(heads_dev, draft_len))
    l_hi, l_lo = split16(l[..., 0].reshape(heads_dev, draft_len))
    stats = jnp.stack(
        [jnp.concatenate([m_hi, m_lo], 1), jnp.concatenate([l_hi, l_lo], 1)], 1
    )
    packed = jnp.concatenate([part_out, stats], 1)
    packed = lax.all_to_all(packed, "seq", 0, 0, tiled=True)
    packed = packed.reshape(seq_count, share, draft_len + 2, 2 * draft_len)
    part_max = join16(packed[:, :, draft_len, :draft_len], packed[:, :, draft_len, draft_len:])
    part_total = join16(
        packed[:, :, draft_len + 1, :draft_len], packed[:, :, draft_len + 1, draft_len:]
    )
    part_sum = packed[:, :, :draft_len, :].astype(jnp.float32)
    final_max = jnp.max(part_max, axis=0)
    factor = jnp.exp2((part_max - final_max[None]) * EXP2_SCALE) * part_total
    final_total = jnp.sum(factor, axis=0)
    final_sum = jnp.sum(part_sum * factor[..., None], axis=0)
    if owner_mode:
        rows_owned = share * draft_len
        owned_query = lax.dynamic_index_in_dim(queries, seq_index, 0, keepdims=True)
        owned_state = (
            final_max.reshape(1, rows_owned, 1),
            jnp.broadcast_to(final_total.reshape(1, rows_owned, 1), (1, rows_owned, HD)),
            final_sum.reshape(1, rows_owned, HD),
        )
        _, owned_total, owned_sum = shared_attend(owned_query, owned_state, owner_blocks)
        attended = (owned_sum / owned_total).reshape(share, draft_len, HD).astype(jnp.bfloat16)
    else:
        attended = (final_sum / final_total[..., None]).astype(jnp.bfloat16)
    attended = jnp.transpose(attended, (1, 0, 2)).reshape(draft_len, share * HD)
    out_group = ("tensor", "seq")
    owners = lax.axis_size("tensor") * seq_count
    columns = out_weight.shape[1] // owners
    product = jnp.dot(attended, out_weight, preferred_element_type=jnp.float32).astype(jnp.bfloat16)
    product = product.reshape(draft_len, owners, columns).transpose(1, 0, 2)
    pieces = lax.all_to_all(product, out_group, 0, 0, tiled=True)
    verified = jnp.sum(pieces.astype(jnp.float32), axis=0).astype(jnp.bfloat16)[None]
    accepted_kv = jnp.take(draft_kv[0], accepted[0], axis=1)[None]
    return (verified, accepted_kv)


def solution(mesh):
    placed = (
        P("req", None, "tensor"),
        P("req", None, None, "tensor"),
        P("req", None, "seq", "tensor"),
        P(None, None, ("req", "seq"), "tensor"),
        P(("tensor", "seq"), None),
        P("req"),
        P(),
        P("req", None),
        P("req", None),
    )
    return jax.shard_map(
        layer,
        mesh=mesh,
        in_specs=placed,
        out_specs=(P("req", None, ("tensor", "seq")), P("req", None, None, "tensor")),
        check_vma=False,
    )
```
